32 devices in a mesh: gx: 4 (over y, core), gy: 8 (over z, x).
Axes of the slice: x: 2, y: 2, z: 4, core: 2. Of those that a mesh axis runs over, the one named last changes fastest.
Arguments:
- initial_heat_values: float32 [16, 128, 1024], P(None, 'gx', 'gy'), may hold values from -5 to 5
- spreading_coefficients: float32 [16, 128, 1024], P(None, 'gx', 'gy'), may hold values from 1 to 16
Outputs:
- advanced: float32 [16, 128, 1024], P(None, 'gx', 'gy')
The draws below stay inside these ranges and needn't reach their ends.
All inputs are finite; a program needn't handle non-finite values.
Results may differ from the reference program's by a relative error of at most 0.0003.
Values sent between devices are 32-bit elements; how exact they have to be, the bound alone decides.
No kernel may reach another device: no remote copies, remote signals or barrier semaphores. Data moves between devices by JAX's collectives and lax.ppermute only.
A program may use at most 64 MiB of HBM per device.

```python
import math
import jax
import jax.numpy as jnp
from jax import lax

PLANES = 16
NX = 128
NY = 1024


def draw_initial_heat_values(key, part):
    rough_part = jax.random.normal(key, (PLANES, NX, NY), jnp.float32)
    return jnp.clip(rough_part, -5.0, 5.0)


def steps_of(key, dims, shards, smallest, high):
    factor_of, own = 1.0, jax.random.fold_in(key, 6)
    for dim, shards_of in shards:
        steps = jnp.exp(jax.random.uniform(jax.random.fold_in(own, dim), (shards_of,), jnp.float32, smallest / len(shards), high / len(shards)))
        factor_of = factor_of * jnp.repeat(steps, dims[dim] // shards_of).reshape([-1 if axis == dim else 1 for axis in range(len(dims))])
    return factor_of


def setup_inputs(seed: int = 0) -> dict:
    streams_of = jax.random.split(jax.random.key(seed), 3)
    return {
        "initial_heat_values": draw_initial_heat_values(jax.random.fold_in(streams_of[2], 71), 0),
        "spreading_coefficients": jnp.clip(jnp.exp(math.log(16.0) - 2.7725887 * jax.random.uniform(streams_of[1], (PLANES, NX, NY), jnp.float32) ** steps_of(streams_of[1], (PLANES, NX, NY), ((1, 4), (2, 8)), -0.2, 0.2)), 1.0, 16.0),
    }


diffusion_number = 1000.0
implicit_weight = 0.5


def tridiagonal_sweep(lower_band, centre, upper_band, right_side):
    ratio_start = 0.0 * (lower_band[0] + centre[0] + upper_band[0])
    value_start = 0.0 * (ratio_start + right_side[0])

    def forward(carried, entries):
        ratio_prev, value_prev = carried
        lower_now, centre_now, upper_now, side_now = entries
        denominator = centre_now - lower_now * ratio_prev
        ratio_now = upper_now / denominator
        value_now = (side_now - lower_now * value_prev) / denominator
        return (ratio_now, value_now), (ratio_now, value_now)

    _, (ratios, values) = lax.scan(forward, (ratio_start, value_start), (lower_band, centre, upper_band, right_side))

    def backward(following, entries):
        ratio_now, value_now = entries
        solved = value_now - ratio_now * following
        return solved, solved

    _, solution = lax.scan(backward, jnp.zeros_like(values[0]), (ratios, values), reverse=True)
    return solution


def curvature_operator_segment(values, conductivity_map, direction):
    leading = jnp.moveaxis(values, direction, 0)
    padded_lines = jnp.pad(leading, [(1, 1)] + [(0, 0)] * (leading.ndim - 1))
    difference = padded_lines[:-2] - 2.0 * leading + padded_lines[2:]
    return conductivity_map * jnp.moveaxis(difference, 0, direction)


def line_solve(half_rate, right_side, direction):
    lead_rate = jnp.moveaxis(half_rate, direction, 0)
    lead_side = jnp.moveaxis(right_side, direction, 0)
    solution = tridiagonal_sweep(-lead_rate, 1.0 + 2.0 * lead_rate, -lead_rate, lead_side)
    return jnp.moveaxis(solution, 0, direction)


def reference(initial_heat_values, spreading_coefficients):
    conductivity_map = diffusion_number * spreading_coefficients
    half_rate = implicit_weight * conductivity_map
    depth_implicit_solve = curvature_operator_segment(initial_heat_values, conductivity_map, 0)
    horizontal_implicit_solve = curvature_operator_segment(initial_heat_values, conductivity_map, 1)
    vertical_implicit_solve = curvature_operator_segment(initial_heat_values, conductivity_map, 2)
    forward_euler_increment = initial_heat_values + horizontal_implicit_solve + vertical_implicit_solve + depth_implicit_solve
    first_pass = line_solve(half_rate, forward_euler_increment - implicit_weight * horizontal_implicit_solve, 1)
    second = line_solve(half_rate, first_pass - implicit_weight * vertical_implicit_solve, 2)
    return line_solve(half_rate, second - implicit_weight * depth_implicit_solve, 0)
```

```python
import jax
import jax.numpy as jnp
from jax import lax
from jax.experimental import pallas as pl
from jax.experimental.pallas import tpu as pltpu
from jax.sharding import PartitionSpec as P

diffusion_number = 1000.0
implicit_weight = 0.5


def padded(block, sides, width):
    for axis, dim in sides:
        count = lax.axis_size(axis)
        forward = [(i, i + 1) for i in range(count - 1)]
        backward = [(target, source) for source, target in forward]
        low = lax.ppermute(
            lax.slice_in_dim(block, block.shape[dim] - width, None, axis=dim), axis, forward
        )
        high = lax.ppermute(lax.slice_in_dim(block, 0, width, axis=dim), axis, backward)
        block = jnp.concatenate([low, block, high], axis=dim)
    return block


def partition_kernel(h_ref, d_ref, out_ref, red_ref, ratio_ref):
    n = h_ref.shape[0]
    ratio = jnp.zeros(h_ref.shape[1:], jnp.float32)
    vb = jnp.zeros_like(ratio)
    vf = jnp.zeros_like(ratio)
    for i in range(1, n - 1):
        hi = h_ref[i]
        denom = 1.0 + 2.0 * hi + hi * ratio
        ratio = -hi / denom
        if i == 1:
            vb = d_ref[i] / denom
            vf = hi / denom
        else:
            vb = (d_ref[i] + hi * vb) / denom
            vf = (hi * vf) / denom
        if i == n - 2:
            vl = hi / denom
        ratio_ref[i] = ratio
        out_ref[0, i] = vb
        out_ref[1, i] = vf
    b, f, l = vb, vf, vl
    out_ref[2, n - 2] = l
    for i in range(n - 3, 0, -1):
        r = ratio_ref[i]
        b = out_ref[0, i] - r * b
        f = out_ref[1, i] - r * f
        l = -r * l
        out_ref[0, i] = b
        out_ref[1, i] = f
        out_ref[2, i] = l
    zero = jnp.zeros_like(ratio)
    for k in range(3):
        out_ref[k, 0] = zero
        out_ref[k, n - 1] = zero
    rh = h_ref[0]
    rt = h_ref[n - 1]
    red_ref[0, 0] = -rh
    red_ref[0, 1] = -rt * out_ref[1, n - 2]
    red_ref[1, 0] = 1.0 + 2.0 * rh - rh * out_ref[1, 1]
    red_ref[1, 1] = 1.0 + 2.0 * rt - rt * out_ref[2, n - 2]
    red_ref[2, 0] = -rh * out_ref[2, 1]
    red_ref[2, 1] = -rt
    red_ref[3, 0] = d_ref[0] + rh * out_ref[0, 1]
    red_ref[3, 1] = d_ref[n - 1] + rt * out_ref[0, n - 2]


def partition_call(h_lines, d_lines):
    n = h_lines.shape[0]
    rest = h_lines.shape[1:]
    return pl.pallas_call(
        partition_kernel,
        out_shape=(
            jax.ShapeDtypeStruct((3, n) + rest, jnp.float32),
            jax.ShapeDtypeStruct((4, 2) + rest, jnp.float32),
        ),
        scratch_shapes=[pltpu_vmem((n,) + rest)],
    )(h_lines, d_lines)


def pltpu_vmem(shape):
    return pltpu.VMEM(shape, jnp.float32)


def reduced_kernel(g_ref, out_ref, ratio_ref):
    count = g_ref.shape[0]
    ratio = None
    value = None
    for j in range(2 * count):
        k, q = divmod(j, 2)
        lower = g_ref[k, 0, q]
        centre = g_ref[k, 1, q]
        upper = g_ref[k, 2, q]
        side = g_ref[k, 3, q]
        if j == 0:
            denom = centre
            value = side / denom
        else:
            denom = centre - lower * ratio
            value = (side - lower * value) / denom
        ratio = upper / denom
        ratio_ref[j] = ratio
        out_ref[k, q] = value
    x = value
    for j in range(2 * count - 2, -1, -1):
        k, q = divmod(j, 2)
        x = out_ref[k, q] - ratio_ref[j] * x
        out_ref[k, q] = x


def reduced_call(gathered):
    count = gathered.shape[0]
    rest = gathered.shape[3:]
    return pl.pallas_call(
        reduced_kernel,
        out_shape=jax.ShapeDtypeStruct((count, 2) + rest, jnp.float32),
        scratch_shapes=[pltpu_vmem((2 * count,) + rest)],
    )(gathered)


def sweep_kernel(h_ref, d_ref, out_ref, ratio_ref):
    n = h_ref.shape[0]
    ratio = None
    value = None
    for i in range(n):
        hi = h_ref[i]
        if i == 0:
            denom = 1.0 + 2.0 * hi
            value = d_ref[i] / denom
        else:
            denom = 1.0 + 2.0 * hi + hi * ratio
            value = (d_ref[i] + hi * value) / denom
        ratio = -hi / denom
        ratio_ref[i] = ratio
        out_ref[i] = value
    x = value
    for i in range(n - 2, -1, -1):
        x = out_ref[i] - ratio_ref[i] * x
        out_ref[i] = x


def sweep_call(h_lines, d_lines):
    return pl.pallas_call(
        sweep_kernel,
        out_shape=jax.ShapeDtypeStruct(h_lines.shape, jnp.float32),
        scratch_shapes=[pltpu_vmem(h_lines.shape)],
    )(h_lines, d_lines)


def distributed_solve(h_lines, d_lines, axis):
    responses, reduced = partition_call(h_lines, d_lines)
    gathered = lax.all_gather(reduced, axis)
    ends = reduced_call(gathered)
    head, tail = lax.dynamic_index_in_dim(ends, lax.axis_index(axis), 0, keepdims=False)
    interior = responses[0, 1:-1] + responses[1, 1:-1] * head + responses[2, 1:-1] * tail
    return jnp.concatenate([head[None], interior, tail[None]], 0)


def per_device(initial_heat_values, spreading_coefficients):
    conductivity_map = diffusion_number * spreading_coefficients
    half_rate = implicit_weight * conductivity_map
    plane_count, row_count, column_count = initial_heat_values.shape
    edge_extended_grid = padded(initial_heat_values, (("gx", 1), ("gy", 2)), 1)
    horizontal_implicit_solve = conductivity_map * (
        edge_extended_grid[:, :-2, 1:-1]
        - 2.0 * initial_heat_values
        + edge_extended_grid[:, 2:, 1:-1]
    )
    vertical_implicit_solve = conductivity_map * (
        edge_extended_grid[:, 1:-1, :-2]
        - 2.0 * initial_heat_values
        + edge_extended_grid[:, 1:-1, 2:]
    )
    depth_edge_extension = jnp.pad(initial_heat_values, ((1, 1), (0, 0), (0, 0)))
    depth_implicit_solve = conductivity_map * (
        depth_edge_extension[:-2] - 2.0 * initial_heat_values + depth_edge_extension[2:]
    )
    forward_euler_increment = (
        initial_heat_values
        + horizontal_implicit_solve
        + vertical_implicit_solve
        + depth_implicit_solve
    )
    first_side = jnp.moveaxis(
        forward_euler_increment - implicit_weight * horizontal_implicit_solve, 1, 0
    )
    first_rate = jnp.moveaxis(half_rate, 1, 0)
    first_pass = jnp.moveaxis(distributed_solve(first_rate, first_side, "gx"), 0, 1)
    second_side = first_pass - implicit_weight * vertical_implicit_solve
    lanes = 128
    groups = plane_count * row_count // lanes
    side_lines = jnp.transpose(second_side, (2, 0, 1)).reshape(column_count, groups, lanes)
    rate_lines = jnp.transpose(half_rate, (2, 0, 1)).reshape(column_count, groups, lanes)
    column_lines = distributed_solve(rate_lines, side_lines, "gy")
    second = jnp.transpose(column_lines.reshape(column_count, plane_count, row_count), (1, 2, 0))
    plane_side = second - implicit_weight * depth_implicit_solve
    return sweep_call(half_rate, plane_side)


def solution(mesh):
    in_specs = (P(None, "gx", "gy"), P(None, "gx", "gy"))
    out_specs = P(None, "gx", "gy")
    return jax.shard_map(
        per_device, mesh=mesh, in_specs=in_specs, out_specs=out_specs, check_vma=False
    )
```

```python
import jax
import jax.numpy as jnp
from jax import lax
from jax.experimental import pallas as pl
from jax.experimental.pallas import tpu as pltpu
from jax.sharding import PartitionSpec as P

diffusion_number = 1000.0
implicit_weight = 0.5


def halos(block, axis, dim):
    count = lax.axis_size(axis)
    forward = [(i, i + 1) for i in range(count - 1)]
    backward = [(target, source) for source, target in forward]
    last = lax.index_in_dim(block, block.shape[dim] - 1, dim, keepdims=False)
    first = lax.index_in_dim(block, 0, dim, keepdims=False)
    low = lax.ppermute(last, axis, forward)
    high = lax.ppermute(first, axis, backward)
    return jnp.expand_dims(low, dim), jnp.expand_dims(high, dim)


def partition_kernel(h_ref, d_ref, out_ref, red_ref, ratio_ref):
    n = h_ref.shape[0]
    ratio = jnp.zeros(h_ref.shape[1:], jnp.float32)
    vb = jnp.zeros_like(ratio)
    vf = jnp.zeros_like(ratio)
    for i in range(1, n - 1):
        hi = h_ref[i]
        denom = 1.0 + 2.0 * hi + hi * ratio
        ratio = -hi / denom
        if i == 1:
            vb = d_ref[i] / denom
            vf = hi / denom
        else:
            vb = (d_ref[i] + hi * vb) / denom
            vf = (hi * vf) / denom
        if i == n - 2:
            vl = hi / denom
        ratio_ref[i] = ratio
        out_ref[0, i] = vb
        out_ref[1, i] = vf
    b, f, l = vb, vf, vl
    out_ref[2, n - 2] = l
    for i in range(n - 3, 0, -1):
        r = ratio_ref[i]
        b = out_ref[0, i] - r * b
        f = out_ref[1, i] - r * f
        l = -r * l
        out_ref[0, i] = b
        out_ref[1, i] = f
        out_ref[2, i] = l
    zero = jnp.zeros_like(ratio)
    for k in range(3):
        out_ref[k, 0] = zero
        out_ref[k, n - 1] = zero
    rh = h_ref[0]
    rt = h_ref[n - 1]
    red_ref[0, 0] = -rh
    red_ref[0, 1] = -rt * out_ref[1, n - 2]
    red_ref[1, 0] = 1.0 + 2.0 * rh - rh * out_ref[1, 1]
    red_ref[1, 1] = 1.0 + 2.0 * rt - rt * out_ref[2, n - 2]
    red_ref[2, 0] = -rh * out_ref[2, 1]
    red_ref[2, 1] = -rt
    red_ref[3, 0] = d_ref[0] + rh * out_ref[0, 1]
    red_ref[3, 1] = d_ref[n - 1] + rt * out_ref[0, n - 2]


def partition_call(h_lines, d_lines):
    n = h_lines.shape[0]
    rest = h_lines.shape[1:]
    return pl.pallas_call(
        partition_kernel,
        out_shape=(
            jax.ShapeDtypeStruct((3, n) + rest, jnp.float32),
            jax.ShapeDtypeStruct((4, 2) + rest, jnp.float32),
        ),
        scratch_shapes=[pltpu_vmem((n,) + rest)],
    )(h_lines, d_lines)


def pltpu_vmem(shape):
    return pltpu.VMEM(shape, jnp.float32)


def reduced_kernel(g_ref, out_ref, ratio_ref):
    count = g_ref.shape[0]
    ratio = None
    value = None
    for j in range(2 * count):
        k, q = divmod(j, 2)
        lower = g_ref[k, 0, q]
        centre = g_ref[k, 1, q]
        upper = g_ref[k, 2, q]
        side = g_ref[k, 3, q]
        if j == 0:
            denom = centre
            value = side / denom
        else:
            denom = centre - lower * ratio
            value = (side - lower * value) / denom
        ratio = upper / denom
        ratio_ref[j] = ratio
        out_ref[k, q] = value
    x = value
    for j in range(2 * count - 2, -1, -1):
        k, q = divmod(j, 2)
        x = out_ref[k, q] - ratio_ref[j] * x
        out_ref[k, q] = x


def reduced_call(gathered):
    count = gathered.shape[0]
    rest = gathered.shape[3:]
    return pl.pallas_call(
        reduced_kernel,
        out_shape=jax.ShapeDtypeStruct((count, 2) + rest, jnp.float32),
        scratch_shapes=[pltpu_vmem((2 * count,) + rest)],
    )(gathered)


def sweep_kernel(h_ref, d_ref, out_ref, ratio_ref):
    n = h_ref.shape[0]
    ratio = None
    value = None
    for i in range(n):
        hi = h_ref[i]
        if i == 0:
            denom = 1.0 + 2.0 * hi
            value = d_ref[i] / denom
        else:
            denom = 1.0 + 2.0 * hi + hi * ratio
            value = (d_ref[i] + hi * value) / denom
        ratio = -hi / denom
        ratio_ref[i] = ratio
        out_ref[i] = value
    x = value
    for i in range(n - 2, -1, -1):
        x = out_ref[i] - ratio_ref[i] * x
        out_ref[i] = x


def sweep_call(h_lines, d_lines):
    return pl.pallas_call(
        sweep_kernel,
        out_shape=jax.ShapeDtypeStruct(h_lines.shape, jnp.float32),
        scratch_shapes=[pltpu_vmem(h_lines.shape)],
    )(h_lines, d_lines)


def distributed_solve(h_lines, d_lines, axis):
    responses, reduced = partition_call(h_lines, d_lines)
    gathered = lax.all_gather(reduced, axis)
    ends = reduced_call(gathered)
    head, tail = lax.dynamic_index_in_dim(ends, lax.axis_index(axis), 0, keepdims=False)
    interior = responses[0, 1:-1] + responses[1, 1:-1] * head + responses[2, 1:-1] * tail
    return jnp.concatenate([head[None], interior, tail[None]], 0)


def per_device(initial_heat_values, spreading_coefficients):
    conductivity_map = diffusion_number * spreading_coefficients
    half_rate = implicit_weight * conductivity_map
    plane_count, row_count, column_count = initial_heat_values.shape
    x_low, x_high = halos(initial_heat_values, "gx", 1)
    y_low, y_high = halos(initial_heat_values, "gy", 2)
    horizontal_implicit_solve = conductivity_map * (
        jnp.concatenate([x_low, initial_heat_values[:, :-1]], 1)
        - 2.0 * initial_heat_values
        + jnp.concatenate([initial_heat_values[:, 1:], x_high], 1)
    )
    vertical_implicit_solve = conductivity_map * (
        jnp.concatenate([y_low, initial_heat_values[:, :, :-1]], 2)
        - 2.0 * initial_heat_values
        + jnp.concatenate([initial_heat_values[:, :, 1:], y_high], 2)
    )
    depth_edge_extension = jnp.pad(initial_heat_values, ((1, 1), (0, 0), (0, 0)))
    depth_implicit_solve = conductivity_map * (
        depth_edge_extension[:-2] - 2.0 * initial_heat_values + depth_edge_extension[2:]
    )
    forward_euler_increment = (
        initial_heat_values
        + horizontal_implicit_solve
        + vertical_implicit_solve
        + depth_implicit_solve
    )
    first_side = jnp.moveaxis(
        forward_euler_increment - implicit_weight * horizontal_implicit_solve, 1, 0
    )
    first_rate = jnp.moveaxis(half_rate, 1, 0)
    first_pass = jnp.moveaxis(distributed_solve(first_rate, first_side, "gx"), 0, 1)
    second_side = first_pass - implicit_weight * vertical_implicit_solve
    lanes = 128
    groups = plane_count * row_count // lanes
    side_lines = jnp.transpose(second_side, (2, 0, 1)).reshape(column_count, groups, lanes)
    rate_lines = jnp.transpose(half_rate, (2, 0, 1)).reshape(column_count, groups, lanes)
    column_lines = distributed_solve(rate_lines, side_lines, "gy")
    second = jnp.transpose(column_lines.reshape(column_count, plane_count, row_count), (1, 2, 0))
    plane_side = second - implicit_weight * depth_implicit_solve
    return sweep_call(half_rate, plane_side)


def solution(mesh):
    in_specs = (P(None, "gx", "gy"), P(None, "gx", "gy"))
    out_specs = P(None, "gx", "gy")
    return jax.shard_map(
        per_device, mesh=mesh, in_specs=in_specs, out_specs=out_specs, check_vma=False
    )
```

```python
import jax
import jax.numpy as jnp
from jax import lax
from jax.experimental import pallas as pl
from jax.experimental.pallas import tpu as pltpu
from jax.sharding import PartitionSpec as P

diffusion_number = 1000.0
implicit_weight = 0.5


def halos(block, axis, dim):
    count = lax.axis_size(axis)
    forward = [(i, i + 1) for i in range(count - 1)]
    backward = [(target, source) for source, target in forward]
    last = lax.index_in_dim(block, block.shape[dim] - 1, dim, keepdims=False)
    first = lax.index_in_dim(block, 0, dim, keepdims=False)
    low = lax.ppermute(last, axis, forward)
    high = lax.ppermute(first, axis, backward)
    return jnp.expand_dims(low, dim), jnp.expand_dims(high, dim)


def partition_kernel(h_ref, d_ref, out_ref, red_ref, ratio_ref):
    n = h_ref.shape[0]
    ratio = jnp.zeros(h_ref.shape[1:], jnp.float32)
    vb = jnp.zeros_like(ratio)
    vf = jnp.zeros_like(ratio)
    for i in range(1, n - 1):
        hi = h_ref[i]
        denom = 1.0 + 2.0 * hi + hi * ratio
        ratio = -hi / denom
        if i == 1:
            vb = d_ref[i] / denom
            vf = hi / denom
        else:
            vb = (d_ref[i] + hi * vb) / denom
            vf = (hi * vf) / denom
        if i == n - 2:
            vl = hi / denom
        ratio_ref[i] = ratio
        out_ref[0, i] = vb
        out_ref[1, i] = vf
    b, f, l = vb, vf, vl
    out_ref[2, n - 2] = l
    for i in range(n - 3, 0, -1):
        r = ratio_ref[i]
        b = out_ref[0, i] - r * b
        f = out_ref[1, i] - r * f
        l = -r * l
        out_ref[0, i] = b
        out_ref[1, i] = f
        out_ref[2, i] = l
    zero = jnp.zeros_like(ratio)
    for k in range(3):
        out_ref[k, 0] = zero
        out_ref[k, n - 1] = zero
    rh = h_ref[0]
    rt = h_ref[n - 1]
    red_ref[0, 0] = -rh
    red_ref[0, 1] = -rt * out_ref[1, n - 2]
    red_ref[1, 0] = 1.0 + 2.0 * rh - rh * out_ref[1, 1]
    red_ref[1, 1] = 1.0 + 2.0 * rt - rt * out_ref[2, n - 2]
    red_ref[2, 0] = -rh * out_ref[2, 1]
    red_ref[2, 1] = -rt
    red_ref[3, 0] = d_ref[0] + rh * out_ref[0, 1]
    red_ref[3, 1] = d_ref[n - 1] + rt * out_ref[0, n - 2]


def partition_call(h_lines, d_lines):
    n = h_lines.shape[0]
    rest = h_lines.shape[1:]
    return pl.pallas_call(
        partition_kernel,
        out_shape=(
            jax.ShapeDtypeStruct((3, n) + rest, jnp.float32),
            jax.ShapeDtypeStruct((4, 2) + rest, jnp.float32),
        ),
        scratch_shapes=[pltpu_vmem((n,) + rest)],
    )(h_lines, d_lines)


def pltpu_vmem(shape):
    return pltpu.VMEM(shape, jnp.float32)


def reduced_kernel(g_ref, out_ref, ratio_ref):
    count = g_ref.shape[0]
    ratio = None
    value = None
    for j in range(2 * count):
        k, q = divmod(j, 2)
        lower = g_ref[k, 0, q]
        centre = g_ref[k, 1, q]
        upper = g_ref[k, 2, q]
        side = g_ref[k, 3, q]
        if j == 0:
            denom = centre
            value = side / denom
        else:
            denom = centre - lower * ratio
            value = (side - lower * value) / denom
        ratio = upper / denom
        ratio_ref[j] = ratio
        out_ref[k, q] = value
    x = value
    for j in range(2 * count - 2, -1, -1):
        k, q = divmod(j, 2)
        x = out_ref[k, q] - ratio_ref[j] * x
        out_ref[k, q] = x


def reduced_call(gathered):
    count = gathered.shape[0]
    rest = gathered.shape[3:]
    return pl.pallas_call(
        reduced_kernel,
        out_shape=jax.ShapeDtypeStruct((count, 2) + rest, jnp.float32),
        scratch_shapes=[pltpu_vmem((2 * count,) + rest)],
    )(gathered)


def sweep_kernel(h_ref, d_ref, out_ref, ratio_ref):
    n = h_ref.shape[0]
    ratio = None
    value = None
    for i in range(n):
        hi = h_ref[i]
        if i == 0:
            denom = 1.0 + 2.0 * hi
            value = d_ref[i] / denom
        else:
            denom = 1.0 + 2.0 * hi + hi * ratio
            value = (d_ref[i] + hi * value) / denom
        ratio = -hi / denom
        ratio_ref[i] = ratio
        out_ref[i] = value
    x = value
    for i in range(n - 2, -1, -1):
        x = out_ref[i] - ratio_ref[i] * x
        out_ref[i] = x


def sweep_call(h_lines, d_lines):
    return pl.pallas_call(
        sweep_kernel,
        out_shape=jax.ShapeDtypeStruct(h_lines.shape, jnp.float32),
        scratch_shapes=[pltpu_vmem(h_lines.shape)],
    )(h_lines, d_lines)


def slot_gather(part, axis):
    slots = jnp.zeros((lax.axis_size(axis),) + part.shape, part.dtype)
    return lax.psum(lax.dynamic_update_index_in_dim(slots, part, lax.axis_index(axis), 0), axis)


def distributed_solve(h_lines, d_lines, axis, by_sum):
    responses, reduced = partition_call(h_lines, d_lines)
    if by_sum:
        gathered = slot_gather(reduced, axis)
    else:
        gathered = lax.all_gather(reduced, axis)
    ends = reduced_call(gathered)
    head, tail = lax.dynamic_index_in_dim(ends, lax.axis_index(axis), 0, keepdims=False)
    interior = responses[0, 1:-1] + responses[1, 1:-1] * head + responses[2, 1:-1] * tail
    return jnp.concatenate([head[None], interior, tail[None]], 0)


def per_device(initial_heat_values, spreading_coefficients):
    conductivity_map = diffusion_number * spreading_coefficients
    half_rate = implicit_weight * conductivity_map
    plane_count, row_count, column_count = initial_heat_values.shape
    x_low, x_high = halos(initial_heat_values, "gx", 1)
    y_low, y_high = halos(initial_heat_values, "gy", 2)
    horizontal_implicit_solve = conductivity_map * (
        jnp.concatenate([x_low, initial_heat_values[:, :-1]], 1)
        - 2.0 * initial_heat_values
        + jnp.concatenate([initial_heat_values[:, 1:], x_high], 1)
    )
    vertical_implicit_solve = conductivity_map * (
        jnp.concatenate([y_low, initial_heat_values[:, :, :-1]], 2)
        - 2.0 * initial_heat_values
        + jnp.concatenate([initial_heat_values[:, :, 1:], y_high], 2)
    )
    depth_edge_extension = jnp.pad(initial_heat_values, ((1, 1), (0, 0), (0, 0)))
    depth_implicit_solve = conductivity_map * (
        depth_edge_extension[:-2] - 2.0 * initial_heat_values + depth_edge_extension[2:]
    )
    forward_euler_increment = (
        initial_heat_values
        + horizontal_implicit_solve
        + vertical_implicit_solve
        + depth_implicit_solve
    )
    first_side = jnp.moveaxis(
        forward_euler_increment - implicit_weight * horizontal_implicit_solve, 1, 0
    )
    first_rate = jnp.moveaxis(half_rate, 1, 0)
    first_pass = jnp.moveaxis(distributed_solve(first_rate, first_side, "gx", False), 0, 1)
    second_side = first_pass - implicit_weight * vertical_implicit_solve
    lanes = 128
    groups = plane_count * row_count // lanes
    side_lines = jnp.transpose(second_side, (2, 0, 1)).reshape(column_count, groups, lanes)
    rate_lines = jnp.transpose(half_rate, (2, 0, 1)).reshape(column_count, groups, lanes)
    column_lines = distributed_solve(rate_lines, side_lines, "gy", True)
    second = jnp.transpose(column_lines.reshape(column_count, plane_count, row_count), (1, 2, 0))
    plane_side = second - implicit_weight * depth_implicit_solve
    return sweep_call(half_rate, plane_side)


def solution(mesh):
    in_specs = (P(None, "gx", "gy"), P(None, "gx", "gy"))
    out_specs = P(None, "gx", "gy")
    return jax.shard_map(
        per_device, mesh=mesh, in_specs=in_specs, out_specs=out_specs, check_vma=False
    )
```

```python
import jax
import jax.numpy as jnp
from jax import lax
from jax.experimental import pallas as pl
from jax.experimental.pallas import tpu as pltpu
from jax.sharding import PartitionSpec as P

diffusion_number = 1000.0
implicit_weight = 0.5


def halos(block, axis, dim):
    count = lax.axis_size(axis)
    forward = [(i, i + 1) for i in range(count - 1)]
    backward = [(target, source) for source, target in forward]
    last = lax.index_in_dim(block, block.shape[dim] - 1, dim, keepdims=False)
    first = lax.index_in_dim(block, 0, dim, keepdims=False)
    low = lax.ppermute(last, axis, forward)
    high = lax.ppermute(first, axis, backward)
    return jnp.expand_dims(low, dim), jnp.expand_dims(high, dim)


def partition_kernel(h_ref, d_ref, out_ref, red_ref, ratio_ref):
    n = h_ref.shape[0]
    ratio = jnp.zeros(h_ref.shape[1:], jnp.float32)
    vb = jnp.zeros_like(ratio)
    vf = jnp.zeros_like(ratio)
    for i in range(1, n - 1):
        hi = h_ref[i]
        denom = 1.0 + 2.0 * hi + hi * ratio
        ratio = -hi / denom
        if i == 1:
            vb = d_ref[i] / denom
            vf = hi / denom
        else:
            vb = (d_ref[i] + hi * vb) / denom
            vf = (hi * vf) / denom
        if i == n - 2:
            vl = hi / denom
        ratio_ref[i] = ratio
        out_ref[0, i] = vb
        out_ref[1, i] = vf
    b, f, l = vb, vf, vl
    out_ref[2, n - 2] = l
    for i in range(n - 3, 0, -1):
        r = ratio_ref[i]
        b = out_ref[0, i] - r * b
        f = out_ref[1, i] - r * f
        l = -r * l
        out_ref[0, i] = b
        out_ref[1, i] = f
        out_ref[2, i] = l
    zero = jnp.zeros_like(ratio)
    for k in range(3):
        out_ref[k, 0] = zero
        out_ref[k, n - 1] = zero
    rh = h_ref[0]
    rt = h_ref[n - 1]
    red_ref[0, 0] = -rh
    red_ref[0, 1] = -rt * out_ref[1, n - 2]
    red_ref[1, 0] = 1.0 + 2.0 * rh - rh * out_ref[1, 1]
    red_ref[1, 1] = 1.0 + 2.0 * rt - rt * out_ref[2, n - 2]
    red_ref[2, 0] = -rh * out_ref[2, 1]
    red_ref[2, 1] = -rt
    red_ref[3, 0] = d_ref[0] + rh * out_ref[0, 1]
    red_ref[3, 1] = d_ref[n - 1] + rt * out_ref[0, n - 2]


def partition_call(h_lines, d_lines):
    n = h_lines.shape[0]
    rest = h_lines.shape[1:]
    return pl.pallas_call(
        partition_kernel,
        out_shape=(
            jax.ShapeDtypeStruct((3, n) + rest, jnp.float32),
            jax.ShapeDtypeStruct((4, 2) + rest, jnp.float32),
        ),
        scratch_shapes=[pltpu_vmem((n,) + rest)],
    )(h_lines, d_lines)


def pltpu_vmem(shape):
    return pltpu.VMEM(shape, jnp.float32)


def reduced_kernel(g_ref, out_ref, ratio_ref):
    count = g_ref.shape[0]
    ratio = None
    value = None
    for j in range(2 * count):
        k, q = divmod(j, 2)
        lower = g_ref[k, 0, q]
        centre = g_ref[k, 1, q]
        upper = g_ref[k, 2, q]
        side = g_ref[k, 3, q]
        if j == 0:
            denom = centre
            value = side / denom
        else:
            denom = centre - lower * ratio
            value = (side - lower * value) / denom
        ratio = upper / denom
        ratio_ref[j] = ratio
        out_ref[k, q] = value
    x = value
    for j in range(2 * count - 2, -1, -1):
        k, q = divmod(j, 2)
        x = out_ref[k, q] - ratio_ref[j] * x
        out_ref[k, q] = x


def reduced_call(gathered):
    count = gathered.shape[0]
    rest = gathered.shape[3:]
    return pl.pallas_call(
        reduced_kernel,
        out_shape=jax.ShapeDtypeStruct((count, 2) + rest, jnp.float32),
        scratch_shapes=[pltpu_vmem((2 * count,) + rest)],
    )(gathered)


def sweep_kernel(h_ref, d_ref, out_ref, ratio_ref):
    n = h_ref.shape[0]
    ratio = None
    value = None
    for i in range(n):
        hi = h_ref[i]
        if i == 0:
            denom = 1.0 + 2.0 * hi
            value = d_ref[i] / denom
        else:
            denom = 1.0 + 2.0 * hi + hi * ratio
            value = (d_ref[i] + hi * value) / denom
        ratio = -hi / denom
        ratio_ref[i] = ratio
        out_ref[i] = value
    x = value
    for i in range(n - 2, -1, -1):
        x = out_ref[i] - ratio_ref[i] * x
        out_ref[i] = x


def sweep_call(h_lines, d_lines):
    return pl.pallas_call(
        sweep_kernel,
        out_shape=jax.ShapeDtypeStruct(h_lines.shape, jnp.float32),
        scratch_shapes=[pltpu_vmem(h_lines.shape)],
    )(h_lines, d_lines)


def doubling_gather(part, axis):
    count = lax.axis_size(axis)
    if count & (count - 1):
        return lax.all_gather(part, axis)
    mine = lax.axis_index(axis)
    held = part[None]
    step = 1
    while step < count:
        other = lax.ppermute(held, axis, [(i, i ^ step) for i in range(count)])
        lower = (mine // step) % 2 == 0
        held = jnp.where(
            lower, jnp.concatenate([held, other], 0), jnp.concatenate([other, held], 0)
        )
        step *= 2
    return held


def distributed_solve(h_lines, d_lines, axis, doubling):
    responses, reduced = partition_call(h_lines, d_lines)
    if doubling:
        gathered = doubling_gather(reduced, axis)
    else:
        gathered = lax.all_gather(reduced, axis)
    ends = reduced_call(gathered)
    head, tail = lax.dynamic_index_in_dim(ends, lax.axis_index(axis), 0, keepdims=False)
    interior = responses[0, 1:-1] + responses[1, 1:-1] * head + responses[2, 1:-1] * tail
    return jnp.concatenate([head[None], interior, tail[None]], 0)


def per_device(initial_heat_values, spreading_coefficients):
    conductivity_map = diffusion_number * spreading_coefficients
    half_rate = implicit_weight * conductivity_map
    plane_count, row_count, column_count = initial_heat_values.shape
    x_low, x_high = halos(initial_heat_values, "gx", 1)
    y_low, y_high = halos(initial_heat_values, "gy", 2)
    horizontal_implicit_solve = conductivity_map * (
        jnp.concatenate([x_low, initial_heat_values[:, :-1]], 1)
        - 2.0 * initial_heat_values
        + jnp.concatenate([initial_heat_values[:, 1:], x_high], 1)
    )
    vertical_implicit_solve = conductivity_map * (
        jnp.concatenate([y_low, initial_heat_values[:, :, :-1]], 2)
        - 2.0 * initial_heat_values
        + jnp.concatenate([initial_heat_values[:, :, 1:], y_high], 2)
    )
    depth_edge_extension = jnp.pad(initial_heat_values, ((1, 1), (0, 0), (0, 0)))
    depth_implicit_solve = conductivity_map * (
        depth_edge_extension[:-2] - 2.0 * initial_heat_values + depth_edge_extension[2:]
    )
    forward_euler_increment = (
        initial_heat_values
        + horizontal_implicit_solve
        + vertical_implicit_solve
        + depth_implicit_solve
    )
    first_side = jnp.moveaxis(
        forward_euler_increment - implicit_weight * horizontal_implicit_solve, 1, 0
    )
    first_rate = jnp.moveaxis(half_rate, 1, 0)
    first_pass = jnp.moveaxis(distributed_solve(first_rate, first_side, "gx", False), 0, 1)
    second_side = first_pass - implicit_weight * vertical_implicit_solve
    lanes = 128
    groups = plane_count * row_count // lanes
    side_lines = jnp.transpose(second_side, (2, 0, 1)).reshape(column_count, groups, lanes)
    rate_lines = jnp.transpose(half_rate, (2, 0, 1)).reshape(column_count, groups, lanes)
    column_lines = distributed_solve(rate_lines, side_lines, "gy", True)
    second = jnp.transpose(column_lines.reshape(column_count, plane_count, row_count), (1, 2, 0))
    plane_side = second - implicit_weight * depth_implicit_solve
    return sweep_call(half_rate, plane_side)


def solution(mesh):
    in_specs = (P(None, "gx", "gy"), P(None, "gx", "gy"))
    out_specs = P(None, "gx", "gy")
    return jax.shard_map(
        per_device, mesh=mesh, in_specs=in_specs, out_specs=out_specs, check_vma=False
    )
```

```python
import jax
import jax.numpy as jnp
from jax import lax
from jax.experimental import pallas as pl
from jax.experimental.pallas import tpu as pltpu
from jax.sharding import PartitionSpec as P

diffusion_number = 1000.0
implicit_weight = 0.5


def halos(block, axis, dim):
    count = lax.axis_size(axis)
    forward = [(i, i + 1) for i in range(count - 1)]
    backward = [(target, source) for source, target in forward]
    last = lax.index_in_dim(block, block.shape[dim] - 1, dim, keepdims=False)
    first = lax.index_in_dim(block, 0, dim, keepdims=False)
    low = lax.ppermute(last, axis, forward)
    high = lax.ppermute(first, axis, backward)
    return jnp.expand_dims(low, dim), jnp.expand_dims(high, dim)


def partition_kernel(h_ref, d_ref, out_ref, red_ref, ratio_ref):
    n = h_ref.shape[0]
    ratio = jnp.zeros(h_ref.shape[1:], jnp.float32)
    vb = jnp.zeros_like(ratio)
    vf = jnp.zeros_like(ratio)
    for i in range(1, n - 1):
        hi = h_ref[i]
        denom = 1.0 + 2.0 * hi + hi * ratio
        ratio = -hi / denom
        if i == 1:
            vb = d_ref[i] / denom
            vf = hi / denom
        else:
            vb = (d_ref[i] + hi * vb) / denom
            vf = (hi * vf) / denom
        if i == n - 2:
            vl = hi / denom
        ratio_ref[i] = ratio
        out_ref[0, i] = vb
        out_ref[1, i] = vf
    b, f, l = vb, vf, vl
    out_ref[2, n - 2] = l
    for i in range(n - 3, 0, -1):
        r = ratio_ref[i]
        b = out_ref[0, i] - r * b
        f = out_ref[1, i] - r * f
        l = -r * l
        out_ref[0, i] = b
        out_ref[1, i] = f
        out_ref[2, i] = l
    zero = jnp.zeros_like(ratio)
    for k in range(3):
        out_ref[k, 0] = zero
        out_ref[k, n - 1] = zero
    rh = h_ref[0]
    rt = h_ref[n - 1]
    red_ref[0, 0] = -rh
    red_ref[0, 1] = -rt * out_ref[1, n - 2]
    red_ref[1, 0] = 1.0 + 2.0 * rh - rh * out_ref[1, 1]
    red_ref[1, 1] = 1.0 + 2.0 * rt - rt * out_ref[2, n - 2]
    red_ref[2, 0] = -rh * out_ref[2, 1]
    red_ref[2, 1] = -rt
    red_ref[3, 0] = d_ref[0] + rh * out_ref[0, 1]
    red_ref[3, 1] = d_ref[n - 1] + rt * out_ref[0, n - 2]


def partition_call(h_lines, d_lines):
    n = h_lines.shape[0]
    rest = h_lines.shape[1:]
    return pl.pallas_call(
        partition_kernel,
        out_shape=(
            jax.ShapeDtypeStruct((3, n) + rest, jnp.float32),
            jax.ShapeDtypeStruct((4, 2) + rest, jnp.float32),
        ),
        scratch_shapes=[pltpu_vmem((n,) + rest)],
    )(h_lines, d_lines)


def pltpu_vmem(shape):
    return pltpu.VMEM(shape, jnp.float32)


def reduced_kernel(g_ref, out_ref, ratio_ref):
    count = g_ref.shape[0]
    ratio = None
    value = None
    for j in range(2 * count):
        k, q = divmod(j, 2)
        lower = g_ref[k, 0, q]
        centre = g_ref[k, 1, q]
        upper = g_ref[k, 2, q]
        side = g_ref[k, 3, q]
        if j == 0:
            denom = centre
            value = side / denom
        else:
            denom = centre - lower * ratio
            value = (side - lower * value) / denom
        ratio = upper / denom
        ratio_ref[j] = ratio
        out_ref[k, q] = value
    x = value
    for j in range(2 * count - 2, -1, -1):
        k, q = divmod(j, 2)
        x = out_ref[k, q] - ratio_ref[j] * x
        out_ref[k, q] = x


def reduced_call(gathered):
    count = gathered.shape[0]
    rest = gathered.shape[3:]
    return pl.pallas_call(
        reduced_kernel,
        out_shape=jax.ShapeDtypeStruct((count, 2) + rest, jnp.float32),
        scratch_shapes=[pltpu_vmem((2 * count,) + rest)],
    )(gathered)


def sweep_kernel(h_ref, d_ref, out_ref, ratio_ref):
    n = h_ref.shape[0]
    ratio = None
    value = None
    for i in range(n):
        hi = h_ref[i]
        if i == 0:
            denom = 1.0 + 2.0 * hi
            value = d_ref[i] / denom
        else:
            denom = 1.0 + 2.0 * hi + hi * ratio
            value = (d_ref[i] + hi * value) / denom
        ratio = -hi / denom
        ratio_ref[i] = ratio
        out_ref[i] = value
    x = value
    for i in range(n - 2, -1, -1):
        x = out_ref[i] - ratio_ref[i] * x
        out_ref[i] = x


def sweep_call(h_lines, d_lines):
    return pl.pallas_call(
        sweep_kernel,
        out_shape=jax.ShapeDtypeStruct(h_lines.shape, jnp.float32),
        scratch_shapes=[pltpu_vmem(h_lines.shape)],
    )(h_lines, d_lines)


def doubling_gather(part, axis):
    count = lax.axis_size(axis)
    if count & (count - 1):
        return lax.all_gather(part, axis)
    mine = lax.axis_index(axis)
    held = part[None]
    step = 1
    while step < count:
        other = lax.ppermute(held, axis, [(i, i ^ step) for i in range(count)])
        lower = (mine // step) % 2 == 0
        held = jnp.where(
            lower, jnp.concatenate([held, other], 0), jnp.concatenate([other, held], 0)
        )
        step *= 2
    return held


def distributed_solve(h_lines, d_lines, axis, doubling):
    responses, reduced = partition_call(h_lines, d_lines)
    if doubling:
        copies = jnp.broadcast_to(reduced[None], (lax.axis_size(axis),) + reduced.shape)
        gathered = lax.all_to_all(copies, axis, 0, 0)
    else:
        gathered = lax.all_gather(reduced, axis)
    ends = reduced_call(gathered)
    head, tail = lax.dynamic_index_in_dim(ends, lax.axis_index(axis), 0, keepdims=False)
    interior = responses[0, 1:-1] + responses[1, 1:-1] * head + responses[2, 1:-1] * tail
    return jnp.concatenate([head[None], interior, tail[None]], 0)


def per_device(initial_heat_values, spreading_coefficients):
    conductivity_map = diffusion_number * spreading_coefficients
    half_rate = implicit_weight * conductivity_map
    plane_count, row_count, column_count = initial_heat_values.shape
    x_low, x_high = halos(initial_heat_values, "gx", 1)
    y_low, y_high = halos(initial_heat_values, "gy", 2)
    horizontal_implicit_solve = conductivity_map * (
        jnp.concatenate([x_low, initial_heat_values[:, :-1]], 1)
        - 2.0 * initial_heat_values
        + jnp.concatenate([initial_heat_values[:, 1:], x_high], 1)
    )
    vertical_implicit_solve = conductivity_map * (
        jnp.concatenate([y_low, initial_heat_values[:, :, :-1]], 2)
        - 2.0 * initial_heat_values
        + jnp.concatenate([initial_heat_values[:, :, 1:], y_high], 2)
    )
    depth_edge_extension = jnp.pad(initial_heat_values, ((1, 1), (0, 0), (0, 0)))
    depth_implicit_solve = conductivity_map * (
        depth_edge_extension[:-2] - 2.0 * initial_heat_values + depth_edge_extension[2:]
    )
    forward_euler_increment = (
        initial_heat_values
        + horizontal_implicit_solve
        + vertical_implicit_solve
        + depth_implicit_solve
    )
    first_side = jnp.moveaxis(
        forward_euler_increment - implicit_weight * horizontal_implicit_solve, 1, 0
    )
    first_rate = jnp.moveaxis(half_rate, 1, 0)
    first_pass = jnp.moveaxis(distributed_solve(first_rate, first_side, "gx", False), 0, 1)
    second_side = first_pass - implicit_weight * vertical_implicit_solve
    lanes = 128
    groups = plane_count * row_count // lanes
    side_lines = jnp.transpose(second_side, (2, 0, 1)).reshape(column_count, groups, lanes)
    rate_lines = jnp.transpose(half_rate, (2, 0, 1)).reshape(column_count, groups, lanes)
    column_lines = distributed_solve(rate_lines, side_lines, "gy", True)
    second = jnp.transpose(column_lines.reshape(column_count, plane_count, row_count), (1, 2, 0))
    plane_side = second - implicit_weight * depth_implicit_solve
    return sweep_call(half_rate, plane_side)


def solution(mesh):
    in_specs = (P(None, "gx", "gy"), P(None, "gx", "gy"))
    out_specs = P(None, "gx", "gy")
    return jax.shard_map(
        per_device, mesh=mesh, in_specs=in_specs, out_specs=out_specs, check_vma=False
    )
```

```python
import jax
import jax.numpy as jnp
from jax import lax
from jax.experimental import pallas as pl
from jax.experimental.pallas import tpu as pltpu
from jax.sharding import PartitionSpec as P

diffusion_number = 1000.0
implicit_weight = 0.5


def halos(block, axis, dim):
    count = lax.axis_size(axis)
    forward = [(i, i + 1) for i in range(count - 1)]
    backward = [(target, source) for source, target in forward]
    last = lax.index_in_dim(block, block.shape[dim] - 1, dim, keepdims=False)
    first = lax.index_in_dim(block, 0, dim, keepdims=False)
    low = lax.ppermute(last, axis, forward)
    high = lax.ppermute(first, axis, backward)
    return jnp.expand_dims(low, dim), jnp.expand_dims(high, dim)


def coefficient_kernel(h_ref, denom_ref, ratio_ref, resp_ref, red_ref):
    n = h_ref.shape[0]
    ratio = jnp.zeros(h_ref.shape[1:], jnp.float32)
    vf = jnp.zeros_like(ratio)
    for i in range(1, n - 1):
        hi = h_ref[i]
        denom = 1.0 + 2.0 * hi + hi * ratio
        ratio = -hi / denom
        if i == 1:
            vf = hi / denom
        else:
            vf = (hi * vf) / denom
        if i == n - 2:
            vl = hi / denom
        denom_ref[i] = denom
        ratio_ref[i] = ratio
        resp_ref[0, i] = vf
    f, l = vf, vl
    resp_ref[1, n - 2] = l
    for i in range(n - 3, 0, -1):
        r = ratio_ref[i]
        f = resp_ref[0, i] - r * f
        l = -r * l
        resp_ref[0, i] = f
        resp_ref[1, i] = l
    zero = jnp.zeros_like(ratio)
    for k in range(2):
        resp_ref[k, 0] = zero
        resp_ref[k, n - 1] = zero
    rh = h_ref[0]
    rt = h_ref[n - 1]
    red_ref[0, 0] = -rh
    red_ref[0, 1] = -rt * resp_ref[0, n - 2]
    red_ref[1, 0] = 1.0 + 2.0 * rh - rh * resp_ref[0, 1]
    red_ref[1, 1] = 1.0 + 2.0 * rt - rt * resp_ref[1, n - 2]
    red_ref[2, 0] = -rh * resp_ref[1, 1]
    red_ref[2, 1] = -rt


def coefficient_call(h_lines):
    n = h_lines.shape[0]
    rest = h_lines.shape[1:]
    return pl.pallas_call(
        coefficient_kernel,
        out_shape=(
            jax.ShapeDtypeStruct((n,) + rest, jnp.float32),
            jax.ShapeDtypeStruct((n,) + rest, jnp.float32),
            jax.ShapeDtypeStruct((2, n) + rest, jnp.float32),
            jax.ShapeDtypeStruct((3, 2) + rest, jnp.float32),
        ),
    )(h_lines)


def side_kernel(h_ref, d_ref, denom_ref, ratio_ref, coef_ref, base_ref, red_ref):
    n = h_ref.shape[0]
    vb = d_ref[1] / denom_ref[1]
    base_ref[1] = vb
    for i in range(2, n - 1):
        vb = (d_ref[i] + h_ref[i] * vb) / denom_ref[i]
        base_ref[i] = vb
    b = vb
    for i in range(n - 3, 0, -1):
        b = base_ref[i] - ratio_ref[i] * b
        base_ref[i] = b
    zero = jnp.zeros_like(b)
    base_ref[0] = zero
    base_ref[n - 1] = zero
    for k in range(3):
        for q in range(2):
            red_ref[k, q] = coef_ref[k, q]
    red_ref[3, 0] = d_ref[0] + h_ref[0] * base_ref[1]
    red_ref[3, 1] = d_ref[n - 1] + h_ref[n - 1] * base_ref[n - 2]


def side_call(h_lines, d_lines, coefficients):
    denom, ratio, _, coef = coefficients
    n = h_lines.shape[0]
    rest = h_lines.shape[1:]
    return pl.pallas_call(
        side_kernel,
        out_shape=(
            jax.ShapeDtypeStruct((n,) + rest, jnp.float32),
            jax.ShapeDtypeStruct((4, 2) + rest, jnp.float32),
        ),
    )(h_lines, d_lines, denom, ratio, coef)


def pltpu_vmem(shape):
    return pltpu.VMEM(shape, jnp.float32)


def reduced_kernel(g_ref, out_ref, ratio_ref):
    count = g_ref.shape[0]
    ratio = None
    value = None
    for j in range(2 * count):
        k, q = divmod(j, 2)
        lower = g_ref[k, 0, q]
        centre = g_ref[k, 1, q]
        upper = g_ref[k, 2, q]
        side = g_ref[k, 3, q]
        if j == 0:
            denom = centre
            value = side / denom
        else:
            denom = centre - lower * ratio
            value = (side - lower * value) / denom
        ratio = upper / denom
        ratio_ref[j] = ratio
        out_ref[k, q] = value
    x = value
    for j in range(2 * count - 2, -1, -1):
        k, q = divmod(j, 2)
        x = out_ref[k, q] - ratio_ref[j] * x
        out_ref[k, q] = x


def reduced_call(gathered):
    count = gathered.shape[0]
    rest = gathered.shape[3:]
    return pl.pallas_call(
        reduced_kernel,
        out_shape=jax.ShapeDtypeStruct((count, 2) + rest, jnp.float32),
        scratch_shapes=[pltpu_vmem((2 * count,) + rest)],
    )(gathered)


def sweep_coefficient_kernel(h_ref, denom_ref, ratio_ref):
    n = h_ref.shape[0]
    ratio = None
    for i in range(n):
        hi = h_ref[i]
        if i == 0:
            denom = 1.0 + 2.0 * hi
        else:
            denom = 1.0 + 2.0 * hi + hi * ratio
        ratio = -hi / denom
        denom_ref[i] = denom
        ratio_ref[i] = ratio


def sweep_side_kernel(h_ref, d_ref, denom_ref, ratio_ref, out_ref):
    n = h_ref.shape[0]
    value = d_ref[0] / denom_ref[0]
    out_ref[0] = value
    for i in range(1, n):
        value = (d_ref[i] + h_ref[i] * value) / denom_ref[i]
        out_ref[i] = value
    x = value
    for i in range(n - 2, -1, -1):
        x = out_ref[i] - ratio_ref[i] * x
        out_ref[i] = x


def sweep_coefficient_call(h_lines):
    shape = jax.ShapeDtypeStruct(h_lines.shape, jnp.float32)
    return pl.pallas_call(sweep_coefficient_kernel, out_shape=(shape, shape))(h_lines)


def sweep_side_call(h_lines, d_lines, coefficients):
    return pl.pallas_call(
        sweep_side_kernel,
        out_shape=jax.ShapeDtypeStruct(h_lines.shape, jnp.float32),
    )(h_lines, d_lines, *coefficients)


def doubling_gather(part, axis):
    count = lax.axis_size(axis)
    if count & (count - 1):
        return lax.all_gather(part, axis)
    mine = lax.axis_index(axis)
    held = part[None]
    step = 1
    while step < count:
        other = lax.ppermute(held, axis, [(i, i ^ step) for i in range(count)])
        lower = (mine // step) % 2 == 0
        held = jnp.where(
            lower, jnp.concatenate([held, other], 0), jnp.concatenate([other, held], 0)
        )
        step *= 2
    return held


def distributed_solve(h_lines, d_lines, coefficients, axis, doubling):
    base, reduced = side_call(h_lines, d_lines, coefficients)
    responses = coefficients[2]
    if doubling:
        gathered = doubling_gather(reduced, axis)
    else:
        gathered = lax.all_gather(reduced, axis)
    ends = reduced_call(gathered)
    head, tail = lax.dynamic_index_in_dim(ends, lax.axis_index(axis), 0, keepdims=False)
    interior = base[1:-1] + responses[0, 1:-1] * head + responses[1, 1:-1] * tail
    return jnp.concatenate([head[None], interior, tail[None]], 0)


def per_device(initial_heat_values, spreading_coefficients):
    conductivity_map = diffusion_number * spreading_coefficients
    half_rate = implicit_weight * conductivity_map
    plane_count, row_count, column_count = initial_heat_values.shape
    x_low, x_high = halos(initial_heat_values, "gx", 1)
    y_low, y_high = halos(initial_heat_values, "gy", 2)
    lanes = 128
    groups = plane_count * row_count // lanes
    first_rate = jnp.moveaxis(half_rate, 1, 0)
    rate_lines = jnp.transpose(half_rate, (2, 0, 1)).reshape(column_count, groups, lanes)
    first_coefficients = coefficient_call(first_rate)
    column_coefficients = coefficient_call(rate_lines)
    plane_coefficients = sweep_coefficient_call(half_rate)
    (x_low, x_high, y_low, y_high), first_coefficients, column_coefficients, plane_coefficients = (
        lax.optimization_barrier(
            (
                (x_low, x_high, y_low, y_high),
                first_coefficients,
                column_coefficients,
                plane_coefficients,
            )
        )
    )
    horizontal_implicit_solve = conductivity_map * (
        jnp.concatenate([x_low, initial_heat_values[:, :-1]], 1)
        - 2.0 * initial_heat_values
        + jnp.concatenate([initial_heat_values[:, 1:], x_high], 1)
    )
    vertical_implicit_solve = conductivity_map * (
        jnp.concatenate([y_low, initial_heat_values[:, :, :-1]], 2)
        - 2.0 * initial_heat_values
        + jnp.concatenate([initial_heat_values[:, :, 1:], y_high], 2)
    )
    depth_edge_extension = jnp.pad(initial_heat_values, ((1, 1), (0, 0), (0, 0)))
    depth_implicit_solve = conductivity_map * (
        depth_edge_extension[:-2] - 2.0 * initial_heat_values + depth_edge_extension[2:]
    )
    forward_euler_increment = (
        initial_heat_values
        + horizontal_implicit_solve
        + vertical_implicit_solve
        + depth_implicit_solve
    )
    first_side = jnp.moveaxis(
        forward_euler_increment - implicit_weight * horizontal_implicit_solve, 1, 0
    )
    first_pass = jnp.moveaxis(
        distributed_solve(first_rate, first_side, first_coefficients, "gx", False), 0, 1
    )
    second_side = first_pass - implicit_weight * vertical_implicit_solve
    side_lines = jnp.transpose(second_side, (2, 0, 1)).reshape(column_count, groups, lanes)
    column_lines = distributed_solve(rate_lines, side_lines, column_coefficients, "gy", True)
    second = jnp.transpose(column_lines.reshape(column_count, plane_count, row_count), (1, 2, 0))
    plane_side = second - implicit_weight * depth_implicit_solve
    return sweep_side_call(half_rate, plane_side, plane_coefficients)


def solution(mesh):
    in_specs = (P(None, "gx", "gy"), P(None, "gx", "gy"))
    out_specs = P(None, "gx", "gy")
    return jax.shard_map(
        per_device, mesh=mesh, in_specs=in_specs, out_specs=out_specs, check_vma=False
    )
```

```python
import jax
import jax.numpy as jnp
from jax import lax
from jax.experimental import pallas as pl
from jax.experimental.pallas import tpu as pltpu
from jax.sharding import PartitionSpec as P

diffusion_number = 1000.0
implicit_weight = 0.5


def halos(block, axis, dim):
    count = lax.axis_size(axis)
    forward = [(i, i + 1) for i in range(count - 1)]
    backward = [(target, source) for source, target in forward]
    last = lax.index_in_dim(block, block.shape[dim] - 1, dim, keepdims=False)
    first = lax.index_in_dim(block, 0, dim, keepdims=False)
    low = lax.ppermute(last, axis, forward)
    high = lax.ppermute(first, axis, backward)
    return jnp.expand_dims(low, dim), jnp.expand_dims(high, dim)


def partition_kernel(h_ref, d_ref, out_ref, red_ref, ratio_ref):
    n = h_ref.shape[0]
    ratio = jnp.zeros(h_ref.shape[1:], jnp.float32)
    vb = jnp.zeros_like(ratio)
    vf = jnp.zeros_like(ratio)
    for i in range(1, n - 1):
        hi = h_ref[i]
        denom = 1.0 + 2.0 * hi + hi * ratio
        ratio = -hi / denom
        if i == 1:
            vb = d_ref[i] / denom
            vf = hi / denom
        else:
            vb = (d_ref[i] + hi * vb) / denom
            vf = (hi * vf) / denom
        if i == n - 2:
            vl = hi / denom
        ratio_ref[i] = ratio
        out_ref[0, i] = vb
        out_ref[1, i] = vf
    b, f, l = vb, vf, vl
    out_ref[2, n - 2] = l
    for i in range(n - 3, 0, -1):
        r = ratio_ref[i]
        b = out_ref[0, i] - r * b
        f = out_ref[1, i] - r * f
        l = -r * l
        out_ref[0, i] = b
        out_ref[1, i] = f
        out_ref[2, i] = l
    zero = jnp.zeros_like(ratio)
    for k in range(3):
        out_ref[k, 0] = zero
        out_ref[k, n - 1] = zero
    rh = h_ref[0]
    rt = h_ref[n - 1]
    red_ref[0, 0] = -rh
    red_ref[0, 1] = -rt * out_ref[1, n - 2]
    red_ref[1, 0] = 1.0 + 2.0 * rh - rh * out_ref[1, 1]
    red_ref[1, 1] = 1.0 + 2.0 * rt - rt * out_ref[2, n - 2]
    red_ref[2, 0] = -rh * out_ref[2, 1]
    red_ref[2, 1] = -rt
    red_ref[3, 0] = d_ref[0] + rh * out_ref[0, 1]
    red_ref[3, 1] = d_ref[n - 1] + rt * out_ref[0, n - 2]


def partition_call(h_lines, d_lines):
    n = h_lines.shape[0]
    rest = h_lines.shape[1:]
    return pl.pallas_call(
        partition_kernel,
        out_shape=(
            jax.ShapeDtypeStruct((3, n) + rest, jnp.float32),
            jax.ShapeDtypeStruct((4, 2) + rest, jnp.float32),
        ),
        scratch_shapes=[pltpu_vmem((n,) + rest)],
    )(h_lines, d_lines)


def pltpu_vmem(shape):
    return pltpu.VMEM(shape, jnp.float32)


def reduced_kernel(g_ref, out_ref, ratio_ref):
    count = g_ref.shape[0]
    ratio = None
    value = None
    for j in range(2 * count):
        k, q = divmod(j, 2)
        lower = g_ref[k, 0, q]
        centre = g_ref[k, 1, q]
        upper = g_ref[k, 2, q]
        side = g_ref[k, 3, q]
        if j == 0:
            denom = centre
            value = side / denom
        else:
            denom = centre - lower * ratio
            value = (side - lower * value) / denom
        ratio = upper / denom
        ratio_ref[j] = ratio
        out_ref[k, q] = value
    x = value
    for j in range(2 * count - 2, -1, -1):
        k, q = divmod(j, 2)
        x = out_ref[k, q] - ratio_ref[j] * x
        out_ref[k, q] = x


def reduced_call(gathered):
    count = gathered.shape[0]
    rest = gathered.shape[3:]
    return pl.pallas_call(
        reduced_kernel,
        out_shape=jax.ShapeDtypeStruct((count, 2) + rest, jnp.float32),
        scratch_shapes=[pltpu_vmem((2 * count,) + rest)],
    )(gathered)


def sweep_kernel(h_ref, d_ref, out_ref, ratio_ref):
    n = h_ref.shape[0]
    ratio = None
    value = None
    for i in range(n):
        hi = h_ref[i]
        if i == 0:
            denom = 1.0 + 2.0 * hi
            value = d_ref[i] / denom
        else:
            denom = 1.0 + 2.0 * hi + hi * ratio
            value = (d_ref[i] + hi * value) / denom
        ratio = -hi / denom
        ratio_ref[i] = ratio
        out_ref[i] = value
    x = value
    for i in range(n - 2, -1, -1):
        x = out_ref[i] - ratio_ref[i] * x
        out_ref[i] = x


def sweep_call(h_lines, d_lines):
    return pl.pallas_call(
        sweep_kernel,
        out_shape=jax.ShapeDtypeStruct(h_lines.shape, jnp.float32),
        scratch_shapes=[pltpu_vmem(h_lines.shape)],
    )(h_lines, d_lines)


def doubling_gather(part, axis):
    count = lax.axis_size(axis)
    if count & (count - 1):
        return lax.all_gather(part, axis)
    mine = lax.axis_index(axis)
    held = part[None]
    step = 1
    while step < count:
        other = lax.ppermute(held, axis, [(i, i ^ step) for i in range(count)])
        lower = (mine // step) % 2 == 0
        held = jnp.where(
            lower, jnp.concatenate([held, other], 0), jnp.concatenate([other, held], 0)
        )
        step *= 2
    return held


def shifted_gather(part, axis):
    count = lax.axis_size(axis)
    received = [part]
    for shift in range(1, count):
        received.append(
            lax.ppermute(part, axis, [(i, (i - shift) % count) for i in range(count)])
        )
    return jnp.roll(jnp.stack(received, 0), lax.axis_index(axis), 0)


def distributed_solve(h_lines, d_lines, axis, doubling):
    responses, reduced = partition_call(h_lines, d_lines)
    if doubling and lax.axis_size(axis) <= 8:
        gathered = shifted_gather(reduced, axis)
    elif doubling:
        gathered = doubling_gather(reduced, axis)
    else:
        gathered = lax.all_gather(reduced, axis)
    ends = reduced_call(gathered)
    head, tail = lax.dynamic_index_in_dim(ends, lax.axis_index(axis), 0, keepdims=False)
    interior = responses[0, 1:-1] + responses[1, 1:-1] * head + responses[2, 1:-1] * tail
    return jnp.concatenate([head[None], interior, tail[None]], 0)


def per_device(initial_heat_values, spreading_coefficients):
    conductivity_map = diffusion_number * spreading_coefficients
    half_rate = implicit_weight * conductivity_map
    plane_count, row_count, column_count = initial_heat_values.shape
    x_low, x_high = halos(initial_heat_values, "gx", 1)
    y_low, y_high = halos(initial_heat_values, "gy", 2)
    horizontal_implicit_solve = conductivity_map * (
        jnp.concatenate([x_low, initial_heat_values[:, :-1]], 1)
        - 2.0 * initial_heat_values
        + jnp.concatenate([initial_heat_values[:, 1:], x_high], 1)
    )
    vertical_implicit_solve = conductivity_map * (
        jnp.concatenate([y_low, initial_heat_values[:, :, :-1]], 2)
        - 2.0 * initial_heat_values
        + jnp.concatenate([initial_heat_values[:, :, 1:], y_high], 2)
    )
    depth_edge_extension = jnp.pad(initial_heat_values, ((1, 1), (0, 0), (0, 0)))
    depth_implicit_solve = conductivity_map * (
        depth_edge_extension[:-2] - 2.0 * initial_heat_values + depth_edge_extension[2:]
    )
    forward_euler_increment = (
        initial_heat_values
        + horizontal_implicit_solve
        + vertical_implicit_solve
        + depth_implicit_solve
    )
    first_side = jnp.moveaxis(
        forward_euler_increment - implicit_weight * horizontal_implicit_solve, 1, 0
    )
    first_rate = jnp.moveaxis(half_rate, 1, 0)
    first_pass = jnp.moveaxis(distributed_solve(first_rate, first_side, "gx", False), 0, 1)
    second_side = first_pass - implicit_weight * vertical_implicit_solve
    lanes = 128
    groups = plane_count * row_count // lanes
    side_lines = jnp.transpose(second_side, (2, 0, 1)).reshape(column_count, groups, lanes)
    rate_lines = jnp.transpose(half_rate, (2, 0, 1)).reshape(column_count, groups, lanes)
    column_lines = distributed_solve(rate_lines, side_lines, "gy", True)
    second = jnp.transpose(column_lines.reshape(column_count, plane_count, row_count), (1, 2, 0))
    plane_side = second - implicit_weight * depth_implicit_solve
    return sweep_call(half_rate, plane_side)


def solution(mesh):
    in_specs = (P(None, "gx", "gy"), P(None, "gx", "gy"))
    out_specs = P(None, "gx", "gy")
    return jax.shard_map(
        per_device, mesh=mesh, in_specs=in_specs, out_specs=out_specs, check_vma=False
    )
```

```python
import jax
import jax.numpy as jnp
from jax import lax
from jax.experimental import pallas as pl
from jax.experimental.pallas import tpu as pltpu
from jax.sharding import PartitionSpec as P

diffusion_number = 1000.0
implicit_weight = 0.5


def halos(block, axis, dim):
    count = lax.axis_size(axis)
    forward = [(i, i + 1) for i in range(count - 1)]
    backward = [(target, source) for source, target in forward]
    last = lax.index_in_dim(block, block.shape[dim] - 1, dim, keepdims=False)
    first = lax.index_in_dim(block, 0, dim, keepdims=False)
    low = lax.ppermute(last, axis, forward)
    high = lax.ppermute(first, axis, backward)
    return jnp.expand_dims(low, dim), jnp.expand_dims(high, dim)


def partition_kernel(h_ref, d_ref, out_ref, red_ref, ratio_ref):
    n = h_ref.shape[0]
    ratio = jnp.zeros(h_ref.shape[1:], jnp.float32)
    vb = jnp.zeros_like(ratio)
    vf = jnp.zeros_like(ratio)
    for i in range(1, n - 1):
        hi = h_ref[i]
        denom = 1.0 + 2.0 * hi + hi * ratio
        ratio = -hi / denom
        if i == 1:
            vb = d_ref[i] / denom
            vf = hi / denom
        else:
            vb = (d_ref[i] + hi * vb) / denom
            vf = (hi * vf) / denom
        if i == n - 2:
            vl = hi / denom
        ratio_ref[i] = ratio
        out_ref[0, i] = vb
        out_ref[1, i] = vf
    b, f, l = vb, vf, vl
    out_ref[2, n - 2] = l
    for i in range(n - 3, 0, -1):
        r = ratio_ref[i]
        b = out_ref[0, i] - r * b
        f = out_ref[1, i] - r * f
        l = -r * l
        out_ref[0, i] = b
        out_ref[1, i] = f
        out_ref[2, i] = l
    zero = jnp.zeros_like(ratio)
    for k in range(3):
        out_ref[k, 0] = zero
        out_ref[k, n - 1] = zero
    rh = h_ref[0]
    rt = h_ref[n - 1]
    red_ref[0, 0] = -rh
    red_ref[0, 1] = -rt * out_ref[1, n - 2]
    red_ref[1, 0] = 1.0 + 2.0 * rh - rh * out_ref[1, 1]
    red_ref[1, 1] = 1.0 + 2.0 * rt - rt * out_ref[2, n - 2]
    red_ref[2, 0] = -rh * out_ref[2, 1]
    red_ref[2, 1] = -rt
    red_ref[3, 0] = d_ref[0] + rh * out_ref[0, 1]
    red_ref[3, 1] = d_ref[n - 1] + rt * out_ref[0, n - 2]


def partition_call(h_lines, d_lines):
    n = h_lines.shape[0]
    rest = h_lines.shape[1:]
    return pl.pallas_call(
        partition_kernel,
        out_shape=(
            jax.ShapeDtypeStruct((3, n) + rest, jnp.float32),
            jax.ShapeDtypeStruct((4, 2) + rest, jnp.float32),
        ),
        scratch_shapes=[pltpu_vmem((n,) + rest)],
    )(h_lines, d_lines)


def pltpu_vmem(shape):
    return pltpu.VMEM(shape, jnp.float32)


def finish_kernel(position_ref, g_ref, responses_ref, out_ref, ratio_ref, ends_ref):
    count = g_ref.shape[0]
    n = responses_ref.shape[1]
    ratio = None
    value = None
    for j in range(2 * count):
        k, q = divmod(j, 2)
        lower = g_ref[k, 0, q]
        centre = g_ref[k, 1, q]
        upper = g_ref[k, 2, q]
        side = g_ref[k, 3, q]
        if j == 0:
            denom = centre
            value = side / denom
        else:
            denom = centre - lower * ratio
            value = (side - lower * value) / denom
        ratio = upper / denom
        ratio_ref[j] = ratio
        ends_ref[j] = value
    x = value
    for j in range(2 * count - 2, -1, -1):
        x = ends_ref[j] - ratio_ref[j] * x
        ends_ref[j] = x
    mine = position_ref[0]
    head = ends_ref[2 * mine]
    tail = ends_ref[2 * mine + 1]
    out_ref[0] = head
    out_ref[n - 1] = tail
    for i in range(1, n - 1):
        out_ref[i] = responses_ref[0, i] + responses_ref[1, i] * head + responses_ref[2, i] * tail


def finish_call(gathered, responses, position):
    count = gathered.shape[0]
    rest = gathered.shape[3:]
    n = responses.shape[1]
    return pl.pallas_call(
        finish_kernel,
        out_shape=jax.ShapeDtypeStruct((n,) + rest, jnp.float32),
        in_specs=[
            pl.BlockSpec(memory_space=pltpu.SMEM),
            pl.BlockSpec(memory_space=pltpu.VMEM),
            pl.BlockSpec(memory_space=pltpu.VMEM),
        ],
        scratch_shapes=[pltpu_vmem((2 * count,) + rest), pltpu_vmem((2 * count,) + rest)],
    )(position, gathered, responses)


def sweep_kernel(h_ref, d_ref, out_ref, ratio_ref):
    n = h_ref.shape[0]
    ratio = None
    value = None
    for i in range(n):
        hi = h_ref[i]
        if i == 0:
            denom = 1.0 + 2.0 * hi
            value = d_ref[i] / denom
        else:
            denom = 1.0 + 2.0 * hi + hi * ratio
            value = (d_ref[i] + hi * value) / denom
        ratio = -hi / denom
        ratio_ref[i] = ratio
        out_ref[i] = value
    x = value
    for i in range(n - 2, -1, -1):
        x = out_ref[i] - ratio_ref[i] * x
        out_ref[i] = x


def sweep_call(h_lines, d_lines):
    return pl.pallas_call(
        sweep_kernel,
        out_shape=jax.ShapeDtypeStruct(h_lines.shape, jnp.float32),
        scratch_shapes=[pltpu_vmem(h_lines.shape)],
    )(h_lines, d_lines)


def doubling_gather(part, axis):
    count = lax.axis_size(axis)
    if count & (count - 1):
        return lax.all_gather(part, axis)
    mine = lax.axis_index(axis)
    held = part[None]
    step = 1
    while step < count:
        other = lax.ppermute(held, axis, [(i, i ^ step) for i in range(count)])
        lower = (mine // step) % 2 == 0
        held = jnp.where(
            lower, jnp.concatenate([held, other], 0), jnp.concatenate([other, held], 0)
        )
        step *= 2
    return held


def distributed_solve(h_lines, d_lines, axis, doubling):
    responses, reduced = partition_call(h_lines, d_lines)
    if doubling:
        gathered = doubling_gather(reduced, axis)
    else:
        gathered = lax.all_gather(reduced, axis)
    position = jnp.reshape(lax.axis_index(axis), (1,)).astype(jnp.int32)
    return finish_call(gathered, responses, position)


def per_device(initial_heat_values, spreading_coefficients):
    conductivity_map = diffusion_number * spreading_coefficients
    half_rate = implicit_weight * conductivity_map
    plane_count, row_count, column_count = initial_heat_values.shape
    x_low, x_high = halos(initial_heat_values, "gx", 1)
    y_low, y_high = halos(initial_heat_values, "gy", 2)
    horizontal_implicit_solve = conductivity_map * (
        jnp.concatenate([x_low, initial_heat_values[:, :-1]], 1)
        - 2.0 * initial_heat_values
        + jnp.concatenate([initial_heat_values[:, 1:], x_high], 1)
    )
    vertical_implicit_solve = conductivity_map * (
        jnp.concatenate([y_low, initial_heat_values[:, :, :-1]], 2)
        - 2.0 * initial_heat_values
        + jnp.concatenate([initial_heat_values[:, :, 1:], y_high], 2)
    )
    depth_edge_extension = jnp.pad(initial_heat_values, ((1, 1), (0, 0), (0, 0)))
    depth_implicit_solve = conductivity_map * (
        depth_edge_extension[:-2] - 2.0 * initial_heat_values + depth_edge_extension[2:]
    )
    forward_euler_increment = (
        initial_heat_values
        + horizontal_implicit_solve
        + vertical_implicit_solve
        + depth_implicit_solve
    )
    first_side = jnp.moveaxis(
        forward_euler_increment - implicit_weight * horizontal_implicit_solve, 1, 0
    )
    first_rate = jnp.moveaxis(half_rate, 1, 0)
    first_pass = jnp.moveaxis(distributed_solve(first_rate, first_side, "gx", False), 0, 1)
    second_side = first_pass - implicit_weight * vertical_implicit_solve
    lanes = 128
    groups = plane_count * row_count // lanes
    side_lines = jnp.transpose(second_side, (2, 0, 1)).reshape(column_count, groups, lanes)
    rate_lines = jnp.transpose(half_rate, (2, 0, 1)).reshape(column_count, groups, lanes)
    column_lines = distributed_solve(rate_lines, side_lines, "gy", True)
    second = jnp.transpose(column_lines.reshape(column_count, plane_count, row_count), (1, 2, 0))
    plane_side = second - implicit_weight * depth_implicit_solve
    return sweep_call(half_rate, plane_side)


def solution(mesh):
    in_specs = (P(None, "gx", "gy"), P(None, "gx", "gy"))
    out_specs = P(None, "gx", "gy")
    return jax.shard_map(
        per_device, mesh=mesh, in_specs=in_specs, out_specs=out_specs, check_vma=False
    )
```

```python
import jax
import jax.numpy as jnp
from jax import lax
from jax.experimental import pallas as pl
from jax.experimental.pallas import tpu as pltpu
from jax.sharding import PartitionSpec as P

diffusion_number = 1000.0
implicit_weight = 0.5


def halos(block, axis, dim):
    count = lax.axis_size(axis)
    forward = [(i, i + 1) for i in range(count - 1)]
    backward = [(target, source) for source, target in forward]
    last = lax.index_in_dim(block, block.shape[dim] - 1, dim, keepdims=False)
    first = lax.index_in_dim(block, 0, dim, keepdims=False)
    low = lax.ppermute(last, axis, forward)
    high = lax.ppermute(first, axis, backward)
    return jnp.expand_dims(low, dim), jnp.expand_dims(high, dim)


def partition_kernel(h_ref, d_ref, *refs):
    if len(refs) == 4:
        edges_ref, out_ref, red_ref, ratio_ref = refs
    else:
        edges_ref = None
        out_ref, red_ref, ratio_ref = refs
    n = h_ref.shape[0]
    ratio = jnp.zeros(h_ref.shape[1:], jnp.float32)
    vb = jnp.zeros_like(ratio)
    vf = jnp.zeros_like(ratio)
    for i in range(1, n - 1):
        hi = h_ref[i]
        denom = 1.0 + 2.0 * hi + hi * ratio
        ratio = -hi / denom
        if i == 1:
            vb = d_ref[i] / denom
            vf = hi / denom
        else:
            vb = (d_ref[i] + hi * vb) / denom
            vf = (hi * vf) / denom
        if i == n - 2:
            vl = hi / denom
        ratio_ref[i] = ratio
        out_ref[0, i] = vb
        out_ref[1, i] = vf
    b, f, l = vb, vf, vl
    out_ref[2, n - 2] = l
    for i in range(n - 3, 0, -1):
        r = ratio_ref[i]
        b = out_ref[0, i] - r * b
        f = out_ref[1, i] - r * f
        l = -r * l
        out_ref[0, i] = b
        out_ref[1, i] = f
        out_ref[2, i] = l
    zero = jnp.zeros_like(ratio)
    for k in range(3):
        out_ref[k, 0] = zero
        out_ref[k, n - 1] = zero
    rh = h_ref[0]
    rt = h_ref[n - 1]
    red_ref[0, 0] = -rh
    red_ref[0, 1] = -rt * out_ref[1, n - 2]
    red_ref[1, 0] = 1.0 + 2.0 * rh - rh * out_ref[1, 1]
    red_ref[1, 1] = 1.0 + 2.0 * rt - rt * out_ref[2, n - 2]
    red_ref[2, 0] = -rh * out_ref[2, 1]
    red_ref[2, 1] = -rt
    red_ref[3, 0] = d_ref[0] + rh * out_ref[0, 1]
    red_ref[3, 1] = d_ref[n - 1] + rt * out_ref[0, n - 2]
    if edges_ref is not None:
        red_ref[4, 0] = edges_ref[0]
        red_ref[4, 1] = edges_ref[1]


def partition_call(h_lines, d_lines, edges):
    n = h_lines.shape[0]
    rest = h_lines.shape[1:]
    operands = (h_lines, d_lines) if edges is None else (h_lines, d_lines, edges)
    rows = 4 if edges is None else 5
    return pl.pallas_call(
        partition_kernel,
        out_shape=(
            jax.ShapeDtypeStruct((3, n) + rest, jnp.float32),
            jax.ShapeDtypeStruct((rows, 2) + rest, jnp.float32),
        ),
        scratch_shapes=[pltpu_vmem((n,) + rest)],
    )(*operands)


def pltpu_vmem(shape):
    return pltpu.VMEM(shape, jnp.float32)


def finish_kernel(position_ref, g_ref, responses_ref, out_ref, ratio_ref, ends_ref):
    count = g_ref.shape[0]
    n = responses_ref.shape[1]
    ratio = None
    value = None
    for j in range(2 * count):
        k, q = divmod(j, 2)
        lower = g_ref[k, 0, q]
        centre = g_ref[k, 1, q]
        upper = g_ref[k, 2, q]
        side = g_ref[k, 3, q]
        if g_ref.shape[1] == 5 and q == 0 and k > 0:
            side = side - lower * g_ref[k - 1, 4, 1]
        if g_ref.shape[1] == 5 and q == 1 and k < count - 1:
            side = side - upper * g_ref[k + 1, 4, 0]
        if j == 0:
            denom = centre
            value = side / denom
        else:
            denom = centre - lower * ratio
            value = (side - lower * value) / denom
        ratio = upper / denom
        ratio_ref[j] = ratio
        ends_ref[j] = value
    x = value
    for j in range(2 * count - 2, -1, -1):
        x = ends_ref[j] - ratio_ref[j] * x
        ends_ref[j] = x
    mine = position_ref[0]
    head = ends_ref[2 * mine]
    tail = ends_ref[2 * mine + 1]
    out_ref[0] = head
    out_ref[n - 1] = tail
    for i in range(1, n - 1):
        out_ref[i] = responses_ref[0, i] + responses_ref[1, i] * head + responses_ref[2, i] * tail


def finish_call(gathered, responses, position):
    count = gathered.shape[0]
    rest = gathered.shape[3:]
    n = responses.shape[1]
    return pl.pallas_call(
        finish_kernel,
        out_shape=jax.ShapeDtypeStruct((n,) + rest, jnp.float32),
        in_specs=[
            pl.BlockSpec(memory_space=pltpu.SMEM),
            pl.BlockSpec(memory_space=pltpu.VMEM),
            pl.BlockSpec(memory_space=pltpu.VMEM),
        ],
        scratch_shapes=[pltpu_vmem((2 * count,) + rest), pltpu_vmem((2 * count,) + rest)],
    )(position, gathered, responses)


def sweep_kernel(h_ref, d_ref, out_ref, ratio_ref):
    n = h_ref.shape[0]
    ratio = None
    value = None
    for i in range(n):
        hi = h_ref[i]
        if i == 0:
            denom = 1.0 + 2.0 * hi
            value = d_ref[i] / denom
        else:
            denom = 1.0 + 2.0 * hi + hi * ratio
            value = (d_ref[i] + hi * value) / denom
        ratio = -hi / denom
        ratio_ref[i] = ratio
        out_ref[i] = value
    x = value
    for i in range(n - 2, -1, -1):
        x = out_ref[i] - ratio_ref[i] * x
        out_ref[i] = x


def sweep_call(h_lines, d_lines):
    return pl.pallas_call(
        sweep_kernel,
        out_shape=jax.ShapeDtypeStruct(h_lines.shape, jnp.float32),
        scratch_shapes=[pltpu_vmem(h_lines.shape)],
    )(h_lines, d_lines)


def doubling_gather(part, axis):
    count = lax.axis_size(axis)
    if count & (count - 1):
        return lax.all_gather(part, axis)
    mine = lax.axis_index(axis)
    held = part[None]
    step = 1
    while step < count:
        other = lax.ppermute(held, axis, [(i, i ^ step) for i in range(count)])
        lower = (mine // step) % 2 == 0
        held = jnp.where(
            lower, jnp.concatenate([held, other], 0), jnp.concatenate([other, held], 0)
        )
        step *= 2
    return held


def distributed_solve(h_lines, d_lines, axis, doubling, edges=None):
    responses, reduced = partition_call(h_lines, d_lines, edges)
    if doubling:
        gathered = doubling_gather(reduced, axis)
    else:
        gathered = lax.all_gather(reduced, axis)
    position = jnp.reshape(lax.axis_index(axis), (1,)).astype(jnp.int32)
    return finish_call(gathered, responses, position)


def per_device(initial_heat_values, spreading_coefficients):
    conductivity_map = diffusion_number * spreading_coefficients
    half_rate = implicit_weight * conductivity_map
    plane_count, row_count, column_count = initial_heat_values.shape
    x_low = jnp.zeros_like(initial_heat_values[:, :1])
    x_high = x_low
    y_low, y_high = halos(initial_heat_values, "gy", 2)
    horizontal_implicit_solve = conductivity_map * (
        jnp.concatenate([x_low, initial_heat_values[:, :-1]], 1)
        - 2.0 * initial_heat_values
        + jnp.concatenate([initial_heat_values[:, 1:], x_high], 1)
    )
    vertical_implicit_solve = conductivity_map * (
        jnp.concatenate([y_low, initial_heat_values[:, :, :-1]], 2)
        - 2.0 * initial_heat_values
        + jnp.concatenate([initial_heat_values[:, :, 1:], y_high], 2)
    )
    depth_edge_extension = jnp.pad(initial_heat_values, ((1, 1), (0, 0), (0, 0)))
    depth_implicit_solve = conductivity_map * (
        depth_edge_extension[:-2] - 2.0 * initial_heat_values + depth_edge_extension[2:]
    )
    forward_euler_increment = (
        initial_heat_values
        + horizontal_implicit_solve
        + vertical_implicit_solve
        + depth_implicit_solve
    )
    first_side = jnp.moveaxis(
        forward_euler_increment - implicit_weight * horizontal_implicit_solve, 1, 0
    )
    first_rate = jnp.moveaxis(half_rate, 1, 0)
    first_pass = jnp.moveaxis(distributed_solve(
            first_rate,
            first_side,
            "gx",
            False,
            jnp.stack([initial_heat_values[:, 0], initial_heat_values[:, row_count - 1]], 0),
        ), 0, 1)
    second_side = first_pass - implicit_weight * vertical_implicit_solve
    lanes = 128
    groups = plane_count * row_count // lanes
    side_lines = jnp.transpose(second_side, (2, 0, 1)).reshape(column_count, groups, lanes)
    rate_lines = jnp.transpose(half_rate, (2, 0, 1)).reshape(column_count, groups, lanes)
    column_lines = distributed_solve(rate_lines, side_lines, "gy", True)
    second = jnp.transpose(column_lines.reshape(column_count, plane_count, row_count), (1, 2, 0))
    plane_side = second - implicit_weight * depth_implicit_solve
    return sweep_call(half_rate, plane_side)


def solution(mesh):
    in_specs = (P(None, "gx", "gy"), P(None, "gx", "gy"))
    out_specs = P(None, "gx", "gy")
    return jax.shard_map(
        per_device, mesh=mesh, in_specs=in_specs, out_specs=out_specs, check_vma=False
    )
```

```python
import jax
import jax.numpy as jnp
from jax import lax
from jax.experimental import pallas as pl
from jax.experimental.pallas import tpu as pltpu
from jax.sharding import PartitionSpec as P

diffusion_number = 1000.0
implicit_weight = 0.5


def halos(block, axis, dim):
    count = lax.axis_size(axis)
    forward = [(i, i + 1) for i in range(count - 1)]
    backward = [(target, source) for source, target in forward]
    last = lax.index_in_dim(block, block.shape[dim] - 1, dim, keepdims=False)
    first = lax.index_in_dim(block, 0, dim, keepdims=False)
    low = lax.ppermute(last, axis, forward)
    high = lax.ppermute(first, axis, backward)
    return jnp.expand_dims(low, dim), jnp.expand_dims(high, dim)


def partition_kernel(h_ref, d_ref, *refs):
    if len(refs) == 4:
        edges_ref, out_ref, red_ref, ratio_ref = refs
    else:
        edges_ref = None
        out_ref, red_ref, ratio_ref = refs
    n = h_ref.shape[0]
    ratio = jnp.zeros(h_ref.shape[1:], jnp.float32)
    vb = jnp.zeros_like(ratio)
    vf = jnp.zeros_like(ratio)
    for i in range(1, n - 1):
        hi = h_ref[i]
        pivot = 1.0 / (1.0 + 2.0 * hi + hi * ratio)
        scaled = hi * pivot
        ratio = -scaled
        if i == 1:
            vb = d_ref[i] * pivot
            vf = scaled
        else:
            vb = (d_ref[i] + hi * vb) * pivot
            vf = scaled * vf
        if i == n - 2:
            vl = scaled
        ratio_ref[i] = ratio
        out_ref[0, i] = vb
        out_ref[1, i] = vf
    b, f, l = vb, vf, vl
    out_ref[2, n - 2] = l
    for i in range(n - 3, 0, -1):
        r = ratio_ref[i]
        b = out_ref[0, i] - r * b
        f = out_ref[1, i] - r * f
        l = -r * l
        out_ref[0, i] = b
        out_ref[1, i] = f
        out_ref[2, i] = l
    zero = jnp.zeros_like(ratio)
    for k in range(3):
        out_ref[k, 0] = zero
        out_ref[k, n - 1] = zero
    rh = h_ref[0]
    rt = h_ref[n - 1]
    red_ref[0, 0] = -rh
    red_ref[0, 1] = -rt * out_ref[1, n - 2]
    red_ref[1, 0] = 1.0 + 2.0 * rh - rh * out_ref[1, 1]
    red_ref[1, 1] = 1.0 + 2.0 * rt - rt * out_ref[2, n - 2]
    red_ref[2, 0] = -rh * out_ref[2, 1]
    red_ref[2, 1] = -rt
    red_ref[3, 0] = d_ref[0] + rh * out_ref[0, 1]
    red_ref[3, 1] = d_ref[n - 1] + rt * out_ref[0, n - 2]
    if edges_ref is not None:
        red_ref[4, 0] = edges_ref[0]
        red_ref[4, 1] = edges_ref[1]


def partition_call(h_lines, d_lines, edges):
    n = h_lines.shape[0]
    rest = h_lines.shape[1:]
    operands = (h_lines, d_lines) if edges is None else (h_lines, d_lines, edges)
    rows = 4 if edges is None else 5
    return pl.pallas_call(
        partition_kernel,
        out_shape=(
            jax.ShapeDtypeStruct((3, n) + rest, jnp.float32),
            jax.ShapeDtypeStruct((rows, 2) + rest, jnp.float32),
        ),
        scratch_shapes=[pltpu_vmem((n,) + rest)],
    )(*operands)


def pltpu_vmem(shape):
    return pltpu.VMEM(shape, jnp.float32)


def finish_kernel(position_ref, g_ref, responses_ref, out_ref, ratio_ref, ends_ref):
    count = g_ref.shape[0]
    n = responses_ref.shape[1]
    ratio = None
    value = None
    for j in range(2 * count):
        k, q = divmod(j, 2)
        lower = g_ref[k, 0, q]
        centre = g_ref[k, 1, q]
        upper = g_ref[k, 2, q]
        side = g_ref[k, 3, q]
        if g_ref.shape[1] == 5 and q == 0 and k > 0:
            side = side - lower * g_ref[k - 1, 4, 1]
        if g_ref.shape[1] == 5 and q == 1 and k < count - 1:
            side = side - upper * g_ref[k + 1, 4, 0]
        if j == 0:
            pivot = 1.0 / centre
            value = side * pivot
        else:
            pivot = 1.0 / (centre - lower * ratio)
            value = (side - lower * value) * pivot
        ratio = upper * pivot
        ratio_ref[j] = ratio
        ends_ref[j] = value
    x = value
    for j in range(2 * count - 2, -1, -1):
        x = ends_ref[j] - ratio_ref[j] * x
        ends_ref[j] = x
    mine = position_ref[0]
    head = ends_ref[2 * mine]
    tail = ends_ref[2 * mine + 1]
    out_ref[0] = head
    out_ref[n - 1] = tail
    for i in range(1, n - 1):
        out_ref[i] = responses_ref[0, i] + responses_ref[1, i] * head + responses_ref[2, i] * tail


def finish_call(gathered, responses, position):
    count = gathered.shape[0]
    rest = gathered.shape[3:]
    n = responses.shape[1]
    return pl.pallas_call(
        finish_kernel,
        out_shape=jax.ShapeDtypeStruct((n,) + rest, jnp.float32),
        in_specs=[
            pl.BlockSpec(memory_space=pltpu.SMEM),
            pl.BlockSpec(memory_space=pltpu.VMEM),
            pl.BlockSpec(memory_space=pltpu.VMEM),
        ],
        scratch_shapes=[pltpu_vmem((2 * count,) + rest), pltpu_vmem((2 * count,) + rest)],
    )(position, gathered, responses)


def sweep_kernel(h_ref, d_ref, out_ref, ratio_ref):
    n = h_ref.shape[0]
    ratio = None
    value = None
    for i in range(n):
        hi = h_ref[i]
        if i == 0:
            pivot = 1.0 / (1.0 + 2.0 * hi)
            value = d_ref[i] * pivot
        else:
            pivot = 1.0 / (1.0 + 2.0 * hi + hi * ratio)
            value = (d_ref[i] + hi * value) * pivot
        ratio = -hi * pivot
        ratio_ref[i] = ratio
        out_ref[i] = value
    x = value
    for i in range(n - 2, -1, -1):
        x = out_ref[i] - ratio_ref[i] * x
        out_ref[i] = x


def sweep_call(h_lines, d_lines):
    return pl.pallas_call(
        sweep_kernel,
        out_shape=jax.ShapeDtypeStruct(h_lines.shape, jnp.float32),
        scratch_shapes=[pltpu_vmem(h_lines.shape)],
    )(h_lines, d_lines)


def doubling_gather(part, axis):
    count = lax.axis_size(axis)
    if count & (count - 1):
        return lax.all_gather(part, axis)
    mine = lax.axis_index(axis)
    held = part[None]
    step = 1
    while step < count:
        other = lax.ppermute(held, axis, [(i, i ^ step) for i in range(count)])
        lower = (mine // step) % 2 == 0
        held = jnp.where(
            lower, jnp.concatenate([held, other], 0), jnp.concatenate([other, held], 0)
        )
        step *= 2
    return held


def distributed_solve(h_lines, d_lines, axis, doubling, edges=None):
    responses, reduced = partition_call(h_lines, d_lines, edges)
    if doubling:
        gathered = doubling_gather(reduced, axis)
    else:
        gathered = lax.all_gather(reduced, axis)
    position = jnp.reshape(lax.axis_index(axis), (1,)).astype(jnp.int32)
    return finish_call(gathered, responses, position)


def per_device(initial_heat_values, spreading_coefficients):
    conductivity_map = diffusion_number * spreading_coefficients
    half_rate = implicit_weight * conductivity_map
    plane_count, row_count, column_count = initial_heat_values.shape
    x_low = jnp.zeros_like(initial_heat_values[:, :1])
    x_high = x_low
    y_low, y_high = halos(initial_heat_values, "gy", 2)
    horizontal_implicit_solve = conductivity_map * (
        jnp.concatenate([x_low, initial_heat_values[:, :-1]], 1)
        - 2.0 * initial_heat_values
        + jnp.concatenate([initial_heat_values[:, 1:], x_high], 1)
    )
    vertical_implicit_solve = conductivity_map * (
        jnp.concatenate([y_low, initial_heat_values[:, :, :-1]], 2)
        - 2.0 * initial_heat_values
        + jnp.concatenate([initial_heat_values[:, :, 1:], y_high], 2)
    )
    depth_edge_extension = jnp.pad(initial_heat_values, ((1, 1), (0, 0), (0, 0)))
    depth_implicit_solve = conductivity_map * (
        depth_edge_extension[:-2] - 2.0 * initial_heat_values + depth_edge_extension[2:]
    )
    forward_euler_increment = (
        initial_heat_values
        + horizontal_implicit_solve
        + vertical_implicit_solve
        + depth_implicit_solve
    )
    first_side = jnp.moveaxis(
        forward_euler_increment - implicit_weight * horizontal_implicit_solve, 1, 0
    )
    first_rate = jnp.moveaxis(half_rate, 1, 0)
    first_pass = jnp.moveaxis(distributed_solve(
            first_rate,
            first_side,
            "gx",
            False,
            jnp.stack([initial_heat_values[:, 0], initial_heat_values[:, row_count - 1]], 0),
        ), 0, 1)
    second_side = first_pass - implicit_weight * vertical_implicit_solve
    lanes = 128
    groups = plane_count * row_count // lanes
    side_lines = jnp.transpose(second_side, (2, 0, 1)).reshape(column_count, groups, lanes)
    rate_lines = jnp.transpose(half_rate, (2, 0, 1)).reshape(column_count, groups, lanes)
    column_lines = distributed_solve(rate_lines, side_lines, "gy", True)
    second = jnp.transpose(column_lines.reshape(column_count, plane_count, row_count), (1, 2, 0))
    plane_side = second - implicit_weight * depth_implicit_solve
    return sweep_call(half_rate, plane_side)


def solution(mesh):
    in_specs = (P(None, "gx", "gy"), P(None, "gx", "gy"))
    out_specs = P(None, "gx", "gy")
    return jax.shard_map(
        per_device, mesh=mesh, in_specs=in_specs, out_specs=out_specs, check_vma=False
    )
```

```python
import functools

import jax
import jax.numpy as jnp
from jax import lax
from jax.experimental import pallas as pl
from jax.experimental.pallas import tpu as pltpu
from jax.sharding import PartitionSpec as P

diffusion_number = 1000.0
implicit_weight = 0.5


def halos(block, axis, dim):
    count = lax.axis_size(axis)
    forward = [(i, i + 1) for i in range(count - 1)]
    backward = [(target, source) for source, target in forward]
    last = lax.index_in_dim(block, block.shape[dim] - 1, dim, keepdims=False)
    first = lax.index_in_dim(block, 0, dim, keepdims=False)
    low = lax.ppermute(last, axis, forward)
    high = lax.ppermute(first, axis, backward)
    return jnp.expand_dims(low, dim), jnp.expand_dims(high, dim)


def line(ref, lead, i, axis):
    if axis == 0:
        return ref[lead + (i,)]
    return ref[lead + (slice(None), i)]


def put(ref, lead, i, value, axis):
    if axis == 0:
        ref[lead + (i,)] = value
    else:
        ref[lead + (slice(None), i)] = value


def partition_kernel(axis, h_ref, d_ref, *refs):
    if len(refs) == 4:
        edges_ref, out_ref, red_ref, ratio_ref = refs
    else:
        edges_ref = None
        out_ref, red_ref, ratio_ref = refs
    n = h_ref.shape[axis]
    ratio = jnp.zeros(ratio_ref.shape[1:], jnp.float32)
    vb = jnp.zeros_like(ratio)
    vf = jnp.zeros_like(ratio)
    for i in range(1, n - 1):
        hi = line(h_ref, (), i, axis)
        denom = 1.0 + 2.0 * hi + hi * ratio
        ratio = -hi / denom
        if i == 1:
            vb = line(d_ref, (), i, axis) / denom
            vf = hi / denom
        else:
            vb = (line(d_ref, (), i, axis) + hi * vb) / denom
            vf = (hi * vf) / denom
        if i == n - 2:
            vl = hi / denom
        ratio_ref[i] = ratio
        put(out_ref, (0,), i, vb, axis)
        put(out_ref, (1,), i, vf, axis)
    b, f, l = vb, vf, vl
    put(out_ref, (2,), n - 2, l, axis)
    for i in range(n - 3, 0, -1):
        r = ratio_ref[i]
        b = line(out_ref, (0,), i, axis) - r * b
        f = line(out_ref, (1,), i, axis) - r * f
        l = -r * l
        put(out_ref, (0,), i, b, axis)
        put(out_ref, (1,), i, f, axis)
        put(out_ref, (2,), i, l, axis)
    zero = jnp.zeros_like(ratio)
    for k in range(3):
        put(out_ref, (k,), 0, zero, axis)
        put(out_ref, (k,), n - 1, zero, axis)
    rh = line(h_ref, (), 0, axis)
    rt = line(h_ref, (), n - 1, axis)
    red_ref[0, 0] = -rh
    red_ref[0, 1] = -rt * line(out_ref, (1,), n - 2, axis)
    red_ref[1, 0] = 1.0 + 2.0 * rh - rh * line(out_ref, (1,), 1, axis)
    red_ref[1, 1] = 1.0 + 2.0 * rt - rt * line(out_ref, (2,), n - 2, axis)
    red_ref[2, 0] = -rh * line(out_ref, (2,), 1, axis)
    red_ref[2, 1] = -rt
    red_ref[3, 0] = line(d_ref, (), 0, axis) + rh * line(out_ref, (0,), 1, axis)
    red_ref[3, 1] = line(d_ref, (), n - 1, axis) + rt * line(out_ref, (0,), n - 2, axis)
    if edges_ref is not None:
        red_ref[4, 0] = edges_ref[0]
        red_ref[4, 1] = edges_ref[1]


def partition_call(h_lines, d_lines, edges, axis):
    n = h_lines.shape[axis]
    rest = h_lines.shape[:axis] + h_lines.shape[axis + 1 :]
    operands = (h_lines, d_lines) if edges is None else (h_lines, d_lines, edges)
    rows = 4 if edges is None else 5
    return pl.pallas_call(
        functools.partial(partition_kernel, axis),
        out_shape=(
            jax.ShapeDtypeStruct((3,) + h_lines.shape, jnp.float32),
            jax.ShapeDtypeStruct((rows, 2) + rest, jnp.float32),
        ),
        scratch_shapes=[pltpu_vmem((n,) + rest)],
    )(*operands)


def pltpu_vmem(shape):
    return pltpu.VMEM(shape, jnp.float32)


def finish_kernel(axis, position_ref, g_ref, responses_ref, out_ref, ratio_ref, ends_ref):
    count = g_ref.shape[0]
    n = responses_ref.shape[axis + 1]
    ratio = None
    value = None
    for j in range(2 * count):
        k, q = divmod(j, 2)
        lower = g_ref[k, 0, q]
        centre = g_ref[k, 1, q]
        upper = g_ref[k, 2, q]
        side = g_ref[k, 3, q]
        if g_ref.shape[1] == 5 and q == 0 and k > 0:
            side = side - lower * g_ref[k - 1, 4, 1]
        if g_ref.shape[1] == 5 and q == 1 and k < count - 1:
            side = side - upper * g_ref[k + 1, 4, 0]
        if j == 0:
            denom = centre
            value = side / denom
        else:
            denom = centre - lower * ratio
            value = (side - lower * value) / denom
        ratio = upper / denom
        ratio_ref[j] = ratio
        ends_ref[j] = value
    x = value
    for j in range(2 * count - 2, -1, -1):
        x = ends_ref[j] - ratio_ref[j] * x
        ends_ref[j] = x
    mine = position_ref[0]
    head = ends_ref[2 * mine]
    tail = ends_ref[2 * mine + 1]
    put(out_ref, (), 0, head, axis)
    put(out_ref, (), n - 1, tail, axis)
    for i in range(1, n - 1):
        put(out_ref, (), i, line(responses_ref, (0,), i, axis) + line(responses_ref, (1,), i, axis) * head + line(responses_ref, (2,), i, axis) * tail, axis)


def finish_call(gathered, responses, position, axis):
    count = gathered.shape[0]
    rest = gathered.shape[3:]
    return pl.pallas_call(
        functools.partial(finish_kernel, axis),
        out_shape=jax.ShapeDtypeStruct(responses.shape[1:], jnp.float32),
        in_specs=[
            pl.BlockSpec(memory_space=pltpu.SMEM),
            pl.BlockSpec(memory_space=pltpu.VMEM),
            pl.BlockSpec(memory_space=pltpu.VMEM),
        ],
        scratch_shapes=[pltpu_vmem((2 * count,) + rest), pltpu_vmem((2 * count,) + rest)],
    )(position, gathered, responses)


def sweep_kernel(h_ref, d_ref, out_ref, ratio_ref):
    n = h_ref.shape[0]
    ratio = None
    value = None
    for i in range(n):
        hi = h_ref[i]
        if i == 0:
            denom = 1.0 + 2.0 * hi
            value = d_ref[i] / denom
        else:
            denom = 1.0 + 2.0 * hi + hi * ratio
            value = (d_ref[i] + hi * value) / denom
        ratio = -hi / denom
        ratio_ref[i] = ratio
        out_ref[i] = value
    x = value
    for i in range(n - 2, -1, -1):
        x = out_ref[i] - ratio_ref[i] * x
        out_ref[i] = x


def sweep_call(h_lines, d_lines):
    return pl.pallas_call(
        sweep_kernel,
        out_shape=jax.ShapeDtypeStruct(h_lines.shape, jnp.float32),
        scratch_shapes=[pltpu_vmem(h_lines.shape)],
    )(h_lines, d_lines)


def doubling_gather(part, axis):
    count = lax.axis_size(axis)
    if count & (count - 1):
        return lax.all_gather(part, axis)
    mine = lax.axis_index(axis)
    held = part[None]
    step = 1
    while step < count:
        other = lax.ppermute(held, axis, [(i, i ^ step) for i in range(count)])
        lower = (mine // step) % 2 == 0
        held = jnp.where(
            lower, jnp.concatenate([held, other], 0), jnp.concatenate([other, held], 0)
        )
        step *= 2
    return held


def distributed_solve(h_lines, d_lines, axis, doubling, edges=None, line_axis=0):
    responses, reduced = partition_call(h_lines, d_lines, edges, line_axis)
    if doubling:
        gathered = doubling_gather(reduced, axis)
    else:
        gathered = lax.all_gather(reduced, axis)
    position = jnp.reshape(lax.axis_index(axis), (1,)).astype(jnp.int32)
    return finish_call(gathered, responses, position, line_axis)


def per_device(initial_heat_values, spreading_coefficients):
    conductivity_map = diffusion_number * spreading_coefficients
    half_rate = implicit_weight * conductivity_map
    plane_count, row_count, column_count = initial_heat_values.shape
    x_low = jnp.zeros_like(initial_heat_values[:, :1])
    x_high = x_low
    y_low, y_high = halos(initial_heat_values, "gy", 2)
    horizontal_implicit_solve = conductivity_map * (
        jnp.concatenate([x_low, initial_heat_values[:, :-1]], 1)
        - 2.0 * initial_heat_values
        + jnp.concatenate([initial_heat_values[:, 1:], x_high], 1)
    )
    vertical_implicit_solve = conductivity_map * (
        jnp.concatenate([y_low, initial_heat_values[:, :, :-1]], 2)
        - 2.0 * initial_heat_values
        + jnp.concatenate([initial_heat_values[:, :, 1:], y_high], 2)
    )
    depth_edge_extension = jnp.pad(initial_heat_values, ((1, 1), (0, 0), (0, 0)))
    depth_implicit_solve = conductivity_map * (
        depth_edge_extension[:-2] - 2.0 * initial_heat_values + depth_edge_extension[2:]
    )
    forward_euler_increment = (
        initial_heat_values
        + horizontal_implicit_solve
        + vertical_implicit_solve
        + depth_implicit_solve
    )
    first_side = forward_euler_increment - implicit_weight * horizontal_implicit_solve
    first_pass = distributed_solve(
        half_rate,
        first_side,
        "gx",
        False,
        jnp.stack([initial_heat_values[:, 0], initial_heat_values[:, row_count - 1]], 0),
        1,
    )
    second_side = first_pass - implicit_weight * vertical_implicit_solve
    lanes = 128
    groups = plane_count * row_count // lanes
    side_lines = jnp.transpose(second_side, (2, 0, 1)).reshape(column_count, groups, lanes)
    rate_lines = jnp.transpose(half_rate, (2, 0, 1)).reshape(column_count, groups, lanes)
    column_lines = distributed_solve(rate_lines, side_lines, "gy", True)
    second = jnp.transpose(column_lines.reshape(column_count, plane_count, row_count), (1, 2, 0))
    plane_side = second - implicit_weight * depth_implicit_solve
    return sweep_call(half_rate, plane_side)


def solution(mesh):
    in_specs = (P(None, "gx", "gy"), P(None, "gx", "gy"))
    out_specs = P(None, "gx", "gy")
    return jax.shard_map(
        per_device, mesh=mesh, in_specs=in_specs, out_specs=out_specs, check_vma=False
    )
```

```python
import jax
import jax.numpy as jnp
from jax import lax
from jax.experimental import pallas as pl
from jax.experimental.pallas import tpu as pltpu
from jax.sharding import PartitionSpec as P

diffusion_number = 1000.0
implicit_weight = 0.5


def halos(block, axis, dim):
    count = lax.axis_size(axis)
    forward = [(i, i + 1) for i in range(count - 1)]
    backward = [(target, source) for source, target in forward]
    last = lax.index_in_dim(block, block.shape[dim] - 1, dim, keepdims=False)
    first = lax.index_in_dim(block, 0, dim, keepdims=False)
    low = lax.ppermute(last, axis, forward)
    high = lax.ppermute(first, axis, backward)
    return jnp.expand_dims(low, dim), jnp.expand_dims(high, dim)


def partition_kernel(h_ref, d_ref, *refs):
    if len(refs) == 4:
        edges_ref, out_ref, red_ref, ratio_ref = refs
    else:
        edges_ref = None
        out_ref, red_ref, ratio_ref = refs
    n = h_ref.shape[0]
    ratio = jnp.zeros(h_ref.shape[1:], jnp.float32)
    vb = jnp.zeros_like(ratio)
    vf = jnp.zeros_like(ratio)
    for i in range(1, n - 1):
        hi = h_ref[i]
        denom = 1.0 + 2.0 * hi + hi * ratio
        ratio = -hi / denom
        if i == 1:
            vb = d_ref[i] / denom
            vf = hi / denom
        else:
            vb = (d_ref[i] + hi * vb) / denom
            vf = (hi * vf) / denom
        if i == n - 2:
            vl = hi / denom
        ratio_ref[i] = ratio
        out_ref[0, i] = vb
        out_ref[1, i] = vf
    b, f, l = vb, vf, vl
    out_ref[2, n - 2] = l
    for i in range(n - 3, 0, -1):
        r = ratio_ref[i]
        b = out_ref[0, i] - r * b
        f = out_ref[1, i] - r * f
        l = -r * l
        out_ref[0, i] = b
        out_ref[1, i] = f
        out_ref[2, i] = l
    zero = jnp.zeros_like(ratio)
    for k in range(3):
        out_ref[k, 0] = zero
        out_ref[k, n - 1] = zero
    rh = h_ref[0]
    rt = h_ref[n - 1]
    red_ref[0, 0] = -rh
    red_ref[0, 1] = -rt * out_ref[1, n - 2]
    red_ref[1, 0] = 1.0 + 2.0 * rh - rh * out_ref[1, 1]
    red_ref[1, 1] = 1.0 + 2.0 * rt - rt * out_ref[2, n - 2]
    red_ref[2, 0] = -rh * out_ref[2, 1]
    red_ref[2, 1] = -rt
    red_ref[3, 0] = d_ref[0] + rh * out_ref[0, 1]
    red_ref[3, 1] = d_ref[n - 1] + rt * out_ref[0, n - 2]
    if edges_ref is not None:
        red_ref[4, 0] = edges_ref[0]
        red_ref[4, 1] = edges_ref[1]


def line_block(size):
    return 8 if size % 8 == 0 and size > 8 else size


def partition_call(h_lines, d_lines, edges):
    n, size, lanes = h_lines.shape
    block = line_block(size)
    rows = 4 if edges is None else 5
    lines = pl.BlockSpec((n, block, lanes), lambda i: (0, i, 0))
    in_specs = [lines, lines]
    operands = (h_lines, d_lines)
    if edges is not None:
        in_specs.append(pl.BlockSpec((2, block, lanes), lambda i: (0, i, 0)))
        operands = operands + (edges,)
    return pl.pallas_call(
        partition_kernel,
        grid=(size // block,),
        in_specs=in_specs,
        out_specs=(
            pl.BlockSpec((3, n, block, lanes), lambda i: (0, 0, i, 0)),
            pl.BlockSpec((rows, 2, block, lanes), lambda i: (0, 0, i, 0)),
        ),
        out_shape=(
            jax.ShapeDtypeStruct((3, n, size, lanes), jnp.float32),
            jax.ShapeDtypeStruct((rows, 2, size, lanes), jnp.float32),
        ),
        scratch_shapes=[pltpu_vmem((n, block, lanes))],
    )(*operands)


def pltpu_vmem(shape):
    return pltpu.VMEM(shape, jnp.float32)


def finish_kernel(position_ref, g_ref, responses_ref, out_ref, ratio_ref, ends_ref):
    count = g_ref.shape[0]
    n = responses_ref.shape[1]
    ratio = None
    value = None
    for j in range(2 * count):
        k, q = divmod(j, 2)
        lower = g_ref[k, 0, q]
        centre = g_ref[k, 1, q]
        upper = g_ref[k, 2, q]
        side = g_ref[k, 3, q]
        if g_ref.shape[1] == 5 and q == 0 and k > 0:
            side = side - lower * g_ref[k - 1, 4, 1]
        if g_ref.shape[1] == 5 and q == 1 and k < count - 1:
            side = side - upper * g_ref[k + 1, 4, 0]
        if j == 0:
            denom = centre
            value = side / denom
        else:
            denom = centre - lower * ratio
            value = (side - lower * value) / denom
        ratio = upper / denom
        ratio_ref[j] = ratio
        ends_ref[j] = value
    x = value
    for j in range(2 * count - 2, -1, -1):
        x = ends_ref[j] - ratio_ref[j] * x
        ends_ref[j] = x
    mine = position_ref[0]
    head = ends_ref[2 * mine]
    tail = ends_ref[2 * mine + 1]
    out_ref[0] = head
    out_ref[n - 1] = tail
    for i in range(1, n - 1):
        out_ref[i] = responses_ref[0, i] + responses_ref[1, i] * head + responses_ref[2, i] * tail


def finish_call(gathered, responses, position):
    count, rows = gathered.shape[:2]
    size, lanes = gathered.shape[3:]
    n = responses.shape[1]
    block = line_block(size)
    return pl.pallas_call(
        finish_kernel,
        grid=(size // block,),
        out_shape=jax.ShapeDtypeStruct((n, size, lanes), jnp.float32),
        in_specs=[
            pl.BlockSpec(memory_space=pltpu.SMEM),
            pl.BlockSpec((count, rows, 2, block, lanes), lambda i: (0, 0, 0, i, 0)),
            pl.BlockSpec((3, n, block, lanes), lambda i: (0, 0, i, 0)),
        ],
        out_specs=pl.BlockSpec((n, block, lanes), lambda i: (0, i, 0)),
        scratch_shapes=[
            pltpu_vmem((2 * count, block, lanes)),
            pltpu_vmem((2 * count, block, lanes)),
        ],
    )(position, gathered, responses)


def sweep_kernel(h_ref, d_ref, out_ref, ratio_ref):
    n = h_ref.shape[0]
    ratio = None
    value = None
    for i in range(n):
        hi = h_ref[i]
        if i == 0:
            denom = 1.0 + 2.0 * hi
            value = d_ref[i] / denom
        else:
            denom = 1.0 + 2.0 * hi + hi * ratio
            value = (d_ref[i] + hi * value) / denom
        ratio = -hi / denom
        ratio_ref[i] = ratio
        out_ref[i] = value
    x = value
    for i in range(n - 2, -1, -1):
        x = out_ref[i] - ratio_ref[i] * x
        out_ref[i] = x


def sweep_call(h_lines, d_lines):
    n, size, lanes = h_lines.shape
    block = line_block(size)
    lines = pl.BlockSpec((n, block, lanes), lambda i: (0, i, 0))
    return pl.pallas_call(
        sweep_kernel,
        grid=(size // block,),
        in_specs=[lines, lines],
        out_specs=lines,
        out_shape=jax.ShapeDtypeStruct(h_lines.shape, jnp.float32),
        scratch_shapes=[pltpu_vmem((n, block, lanes))],
    )(h_lines, d_lines)


def doubling_gather(part, axis):
    count = lax.axis_size(axis)
    if count & (count - 1):
        return lax.all_gather(part, axis)
    mine = lax.axis_index(axis)
    held = part[None]
    step = 1
    while step < count:
        other = lax.ppermute(held, axis, [(i, i ^ step) for i in range(count)])
        lower = (mine // step) % 2 == 0
        held = jnp.where(
            lower, jnp.concatenate([held, other], 0), jnp.concatenate([other, held], 0)
        )
        step *= 2
    return held


def distributed_solve(h_lines, d_lines, axis, doubling, edges=None):
    responses, reduced = partition_call(h_lines, d_lines, edges)
    if doubling:
        gathered = doubling_gather(reduced, axis)
    else:
        gathered = lax.all_gather(reduced, axis)
    position = jnp.reshape(lax.axis_index(axis), (1,)).astype(jnp.int32)
    return finish_call(gathered, responses, position)


def per_device(initial_heat_values, spreading_coefficients):
    conductivity_map = diffusion_number * spreading_coefficients
    half_rate = implicit_weight * conductivity_map
    plane_count, row_count, column_count = initial_heat_values.shape
    x_low = jnp.zeros_like(initial_heat_values[:, :1])
    x_high = x_low
    y_low, y_high = halos(initial_heat_values, "gy", 2)
    horizontal_implicit_solve = conductivity_map * (
        jnp.concatenate([x_low, initial_heat_values[:, :-1]], 1)
        - 2.0 * initial_heat_values
        + jnp.concatenate([initial_heat_values[:, 1:], x_high], 1)
    )
    vertical_implicit_solve = conductivity_map * (
        jnp.concatenate([y_low, initial_heat_values[:, :, :-1]], 2)
        - 2.0 * initial_heat_values
        + jnp.concatenate([initial_heat_values[:, :, 1:], y_high], 2)
    )
    depth_edge_extension = jnp.pad(initial_heat_values, ((1, 1), (0, 0), (0, 0)))
    depth_implicit_solve = conductivity_map * (
        depth_edge_extension[:-2] - 2.0 * initial_heat_values + depth_edge_extension[2:]
    )
    forward_euler_increment = (
        initial_heat_values
        + horizontal_implicit_solve
        + vertical_implicit_solve
        + depth_implicit_solve
    )
    first_side = jnp.moveaxis(
        forward_euler_increment - implicit_weight * horizontal_implicit_solve, 1, 0
    )
    first_rate = jnp.moveaxis(half_rate, 1, 0)
    first_pass = jnp.moveaxis(distributed_solve(
            first_rate,
            first_side,
            "gx",
            False,
            jnp.stack([initial_heat_values[:, 0], initial_heat_values[:, row_count - 1]], 0),
        ), 0, 1)
    second_side = first_pass - implicit_weight * vertical_implicit_solve
    lanes = 128
    groups = plane_count * row_count // lanes
    side_lines = jnp.transpose(second_side, (2, 0, 1)).reshape(column_count, groups, lanes)
    rate_lines = jnp.transpose(half_rate, (2, 0, 1)).reshape(column_count, groups, lanes)
    column_lines = distributed_solve(rate_lines, side_lines, "gy", True)
    second = jnp.transpose(column_lines.reshape(column_count, plane_count, row_count), (1, 2, 0))
    plane_side = second - implicit_weight * depth_implicit_solve
    return sweep_call(half_rate, plane_side)


def solution(mesh):
    in_specs = (P(None, "gx", "gy"), P(None, "gx", "gy"))
    out_specs = P(None, "gx", "gy")
    return jax.shard_map(
        per_device, mesh=mesh, in_specs=in_specs, out_specs=out_specs, check_vma=False
    )
```

```python
import jax
import jax.numpy as jnp
from jax import lax
from jax.experimental import pallas as pl
from jax.experimental.pallas import tpu as pltpu
from jax.sharding import PartitionSpec as P

diffusion_number = 1000.0
implicit_weight = 0.5


def halos(block, axis, dim):
    count = lax.axis_size(axis)
    forward = [(i, i + 1) for i in range(count - 1)]
    backward = [(target, source) for source, target in forward]
    last = lax.index_in_dim(block, block.shape[dim] - 1, dim, keepdims=False)
    first = lax.index_in_dim(block, 0, dim, keepdims=False)
    low = lax.ppermute(last, axis, forward)
    high = lax.ppermute(first, axis, backward)
    return jnp.expand_dims(low, dim), jnp.expand_dims(high, dim)


def partition_kernel(h_ref, d_ref, *refs):
    if len(refs) == 4:
        edges_ref, out_ref, red_ref, ratio_ref = refs
    else:
        edges_ref = None
        out_ref, red_ref, ratio_ref = refs
    n = h_ref.shape[0]
    ratio = jnp.zeros(h_ref.shape[1:], jnp.float32)
    vb = jnp.zeros_like(ratio)
    vf = jnp.zeros_like(ratio)
    for i in range(1, n - 1):
        hi = h_ref[i]
        denom = 1.0 + 2.0 * hi + hi * ratio
        ratio = -hi / denom
        if i == 1:
            vb = d_ref[i] / denom
            vf = hi / denom
        else:
            vb = (d_ref[i] + hi * vb) / denom
            vf = (hi * vf) / denom
        if i == n - 2:
            vl = hi / denom
        ratio_ref[i] = ratio
        out_ref[0, i] = vb
        out_ref[1, i] = vf
    b, f, l = vb, vf, vl
    out_ref[2, n - 2] = l
    for i in range(n - 3, 0, -1):
        r = ratio_ref[i]
        b = out_ref[0, i] - r * b
        f = out_ref[1, i] - r * f
        l = -r * l
        out_ref[0, i] = b
        out_ref[1, i] = f
        out_ref[2, i] = l
    zero = jnp.zeros_like(ratio)
    for k in range(3):
        out_ref[k, 0] = zero
        out_ref[k, n - 1] = zero
    rh = h_ref[0]
    rt = h_ref[n - 1]
    red_ref[0, 0] = -rh
    red_ref[0, 1] = -rt * out_ref[1, n - 2]
    red_ref[1, 0] = 1.0 + 2.0 * rh - rh * out_ref[1, 1]
    red_ref[1, 1] = 1.0 + 2.0 * rt - rt * out_ref[2, n - 2]
    red_ref[2, 0] = -rh * out_ref[2, 1]
    red_ref[2, 1] = -rt
    red_ref[3, 0] = d_ref[0] + rh * out_ref[0, 1]
    red_ref[3, 1] = d_ref[n - 1] + rt * out_ref[0, n - 2]
    if edges_ref is not None:
        red_ref[4, 0] = edges_ref[0]
        red_ref[4, 1] = edges_ref[1]


def partition_call(h_lines, d_lines, edges):
    n = h_lines.shape[0]
    rest = h_lines.shape[1:]
    operands = (h_lines, d_lines) if edges is None else (h_lines, d_lines, edges)
    rows = 4 if edges is None else 5
    return pl.pallas_call(
        partition_kernel,
        out_shape=(
            jax.ShapeDtypeStruct((3, n) + rest, jnp.float32),
            jax.ShapeDtypeStruct((rows, 2) + rest, jnp.float32),
        ),
        scratch_shapes=[pltpu_vmem((n,) + rest)],
    )(*operands)


def pltpu_vmem(shape):
    return pltpu.VMEM(shape, jnp.float32)


def finish_kernel(position_ref, g_ref, responses_ref, out_ref, ratio_ref, ends_ref):
    count = g_ref.shape[0]
    n = responses_ref.shape[1]
    ratio = None
    value = None
    for j in range(2 * count):
        k, q = divmod(j, 2)
        lower = g_ref[k, 0, q]
        centre = g_ref[k, 1, q]
        upper = g_ref[k, 2, q]
        side = g_ref[k, 3, q]
        if g_ref.shape[1] == 5 and q == 0 and k > 0:
            side = side - lower * g_ref[k - 1, 4, 1]
        if g_ref.shape[1] == 5 and q == 1 and k < count - 1:
            side = side - upper * g_ref[k + 1, 4, 0]
        if j == 0:
            denom = centre
            value = side / denom
        else:
            denom = centre - lower * ratio
            value = (side - lower * value) / denom
        ratio = upper / denom
        ratio_ref[j] = ratio
        ends_ref[j] = value
    x = value
    for j in range(2 * count - 2, -1, -1):
        x = ends_ref[j] - ratio_ref[j] * x
        ends_ref[j] = x
    mine = position_ref[0]
    head = ends_ref[2 * mine]
    tail = ends_ref[2 * mine + 1]
    out_ref[0] = head
    out_ref[n - 1] = tail
    for i in range(1, n - 1):
        out_ref[i] = responses_ref[0, i] + responses_ref[1, i] * head + responses_ref[2, i] * tail


def finish_call(gathered, responses, position):
    count = gathered.shape[0]
    rest = gathered.shape[3:]
    n = responses.shape[1]
    return pl.pallas_call(
        finish_kernel,
        out_shape=jax.ShapeDtypeStruct((n,) + rest, jnp.float32),
        in_specs=[
            pl.BlockSpec(memory_space=pltpu.SMEM),
            pl.BlockSpec(memory_space=pltpu.VMEM),
            pl.BlockSpec(memory_space=pltpu.VMEM),
        ],
        scratch_shapes=[pltpu_vmem((2 * count,) + rest), pltpu_vmem((2 * count,) + rest)],
    )(position, gathered, responses)


def sweep_kernel(h_ref, d_ref, out_ref, ratio_ref):
    n = h_ref.shape[0]
    ratio = None
    value = None
    for i in range(n):
        hi = h_ref[i]
        if i == 0:
            denom = 1.0 + 2.0 * hi
            value = d_ref[i] / denom
        else:
            denom = 1.0 + 2.0 * hi + hi * ratio
            value = (d_ref[i] + hi * value) / denom
        ratio = -hi / denom
        ratio_ref[i] = ratio
        out_ref[i] = value
    x = value
    for i in range(n - 2, -1, -1):
        x = out_ref[i] - ratio_ref[i] * x
        out_ref[i] = x


def sweep_call(h_lines, d_lines):
    return pl.pallas_call(
        sweep_kernel,
        out_shape=jax.ShapeDtypeStruct(h_lines.shape, jnp.float32),
        scratch_shapes=[pltpu_vmem(h_lines.shape)],
    )(h_lines, d_lines)


def doubling_gather(part, axis):
    count = lax.axis_size(axis)
    if count & (count - 1):
        return lax.all_gather(part, axis)
    mine = lax.axis_index(axis)
    held = part[None]
    step = 1
    while step < count:
        other = lax.ppermute(held, axis, [(i, i ^ step) for i in range(count)])
        lower = (mine // step) % 2 == 0
        held = jnp.where(
            lower, jnp.concatenate([held, other], 0), jnp.concatenate([other, held], 0)
        )
        step *= 2
    return held


def distributed_solve(h_lines, d_lines, axis, doubling, edges=None):
    responses, reduced = partition_call(h_lines, d_lines, edges)
    if doubling:
        gathered = doubling_gather(reduced, axis)
    else:
        gathered = lax.all_gather(reduced, axis)
    position = jnp.reshape(lax.axis_index(axis), (1,)).astype(jnp.int32)
    return finish_call(gathered, responses, position)


def per_device(initial_heat_values, spreading_coefficients):
    conductivity_map = diffusion_number * spreading_coefficients
    half_rate = implicit_weight * conductivity_map
    plane_count, row_count, column_count = initial_heat_values.shape
    x_low = jnp.zeros_like(initial_heat_values[:, :1])
    x_high = x_low
    y_low, y_high = halos(initial_heat_values, "gy", 2)
    horizontal_implicit_solve = conductivity_map * (
        jnp.concatenate([x_low, initial_heat_values[:, :-1]], 1)
        - 2.0 * initial_heat_values
        + jnp.concatenate([initial_heat_values[:, 1:], x_high], 1)
    )
    vertical_implicit_solve = conductivity_map * (
        jnp.concatenate([y_low, initial_heat_values[:, :, :-1]], 2)
        - 2.0 * initial_heat_values
        + jnp.concatenate([initial_heat_values[:, :, 1:], y_high], 2)
    )
    depth_edge_extension = jnp.pad(initial_heat_values, ((1, 1), (0, 0), (0, 0)))
    depth_implicit_solve = conductivity_map * (
        depth_edge_extension[:-2] - 2.0 * initial_heat_values + depth_edge_extension[2:]
    )
    forward_euler_increment = (
        initial_heat_values
        + horizontal_implicit_solve
        + vertical_implicit_solve
        + depth_implicit_solve
    )
    first_side = jnp.moveaxis(
        forward_euler_increment - implicit_weight * horizontal_implicit_solve, 1, 0
    )
    first_rate = jnp.moveaxis(half_rate, 1, 0)
    first_pass = jnp.moveaxis(distributed_solve(
            first_rate,
            first_side,
            "gx",
            True,
            jnp.stack([initial_heat_values[:, 0], initial_heat_values[:, row_count - 1]], 0),
        ), 0, 1)
    second_side = first_pass - implicit_weight * vertical_implicit_solve
    lanes = 128
    groups = plane_count * row_count // lanes
    side_lines = jnp.transpose(second_side, (2, 0, 1)).reshape(column_count, groups, lanes)
    rate_lines = jnp.transpose(half_rate, (2, 0, 1)).reshape(column_count, groups, lanes)
    column_lines = distributed_solve(rate_lines, side_lines, "gy", True)
    second = jnp.transpose(column_lines.reshape(column_count, plane_count, row_count), (1, 2, 0))
    plane_side = second - implicit_weight * depth_implicit_solve
    return sweep_call(half_rate, plane_side)


def solution(mesh):
    in_specs = (P(None, "gx", "gy"), P(None, "gx", "gy"))
    out_specs = P(None, "gx", "gy")
    return jax.shard_map(
        per_device, mesh=mesh, in_specs=in_specs, out_specs=out_specs, check_vma=False
    )
```

```python
import jax
import jax.numpy as jnp
from jax import lax
from jax.experimental import pallas as pl
from jax.experimental.pallas import tpu as pltpu
from jax.sharding import PartitionSpec as P

diffusion_number = 1000.0
implicit_weight = 0.5


def halos(block, axis, dim):
    count = lax.axis_size(axis)
    forward = [(i, i + 1) for i in range(count - 1)]
    backward = [(target, source) for source, target in forward]
    last = lax.index_in_dim(block, block.shape[dim] - 1, dim, keepdims=False)
    first = lax.index_in_dim(block, 0, dim, keepdims=False)
    low = lax.ppermute(last, axis, forward)
    high = lax.ppermute(first, axis, backward)
    return jnp.expand_dims(low, dim), jnp.expand_dims(high, dim)


def partition_kernel(h_ref, d_ref, *refs):
    if len(refs) == 4:
        edges_ref, out_ref, red_ref, ratio_ref = refs
    else:
        edges_ref = None
        out_ref, red_ref, ratio_ref = refs
    n = h_ref.shape[0]
    ratio = jnp.zeros(h_ref.shape[1:], jnp.float32)
    vb = jnp.zeros_like(ratio)
    vf = jnp.zeros_like(ratio)
    for i in range(1, n - 1):
        hi = h_ref[i]
        denom = 1.0 + 2.0 * hi + hi * ratio
        ratio = -hi / denom
        if i == 1:
            vb = d_ref[i] / denom
            vf = hi / denom
        else:
            vb = (d_ref[i] + hi * vb) / denom
            vf = (hi * vf) / denom
        if i == n - 2:
            vl = hi / denom
        ratio_ref[i] = ratio
        out_ref[0, i] = vb
        out_ref[1, i] = vf
    b, f, l = vb, vf, vl
    out_ref[2, n - 2] = l
    for i in range(n - 3, 0, -1):
        r = ratio_ref[i]
        b = out_ref[0, i] - r * b
        f = out_ref[1, i] - r * f
        l = -r * l
        out_ref[0, i] = b
        out_ref[1, i] = f
        out_ref[2, i] = l
    zero = jnp.zeros_like(ratio)
    for k in range(3):
        out_ref[k, 0] = zero
        out_ref[k, n - 1] = zero
    rh = h_ref[0]
    rt = h_ref[n - 1]
    red_ref[0, 0] = -rh
    red_ref[0, 1] = -rt * out_ref[1, n - 2]
    red_ref[1, 0] = 1.0 + 2.0 * rh - rh * out_ref[1, 1]
    red_ref[1, 1] = 1.0 + 2.0 * rt - rt * out_ref[2, n - 2]
    red_ref[2, 0] = -rh * out_ref[2, 1]
    red_ref[2, 1] = -rt
    red_ref[3, 0] = d_ref[0] + rh * out_ref[0, 1]
    red_ref[3, 1] = d_ref[n - 1] + rt * out_ref[0, n - 2]
    if edges_ref is not None:
        red_ref[4, 0] = edges_ref[0]
        red_ref[4, 1] = edges_ref[1]


def partition_call(h_lines, d_lines, edges):
    n = h_lines.shape[0]
    rest = h_lines.shape[1:]
    operands = (h_lines, d_lines) if edges is None else (h_lines, d_lines, edges)
    rows = 4 if edges is None else 5
    return pl.pallas_call(
        partition_kernel,
        out_shape=(
            jax.ShapeDtypeStruct((3, n) + rest, jnp.float32),
            jax.ShapeDtypeStruct((rows, 2) + rest, jnp.float32),
        ),
        scratch_shapes=[pltpu_vmem((n,) + rest)],
    )(*operands)


def pltpu_vmem(shape):
    return pltpu.VMEM(shape, jnp.float32)


def finish_kernel(position_ref, g_ref, responses_ref, out_ref, ratio_ref, ends_ref):
    count = g_ref.shape[0]
    n = responses_ref.shape[1]
    ratio = None
    value = None
    for j in range(2 * count):
        k, q = divmod(j, 2)
        lower = g_ref[k, 0, q]
        centre = g_ref[k, 1, q]
        upper = g_ref[k, 2, q]
        side = g_ref[k, 3, q]
        if g_ref.shape[1] == 5 and q == 0 and k > 0:
            side = side - lower * g_ref[k - 1, 4, 1]
        if g_ref.shape[1] == 5 and q == 1 and k < count - 1:
            side = side - upper * g_ref[k + 1, 4, 0]
        if j == 0:
            denom = centre
            value = side / denom
        else:
            denom = centre - lower * ratio
            value = (side - lower * value) / denom
        ratio = upper / denom
        ratio_ref[j] = ratio
        ends_ref[j] = value
    x = value
    for j in range(2 * count - 2, -1, -1):
        x = ends_ref[j] - ratio_ref[j] * x
        ends_ref[j] = x
    mine = position_ref[0]
    head = ends_ref[2 * mine]
    tail = ends_ref[2 * mine + 1]
    out_ref[0] = head
    out_ref[n - 1] = tail
    for i in range(1, n - 1):
        out_ref[i] = responses_ref[0, i] + responses_ref[1, i] * head + responses_ref[2, i] * tail


def finish_call(gathered, responses, position):
    count = gathered.shape[0]
    rest = gathered.shape[3:]
    n = responses.shape[1]
    return pl.pallas_call(
        finish_kernel,
        out_shape=jax.ShapeDtypeStruct((n,) + rest, jnp.float32),
        in_specs=[
            pl.BlockSpec(memory_space=pltpu.SMEM),
            pl.BlockSpec(memory_space=pltpu.VMEM),
            pl.BlockSpec(memory_space=pltpu.VMEM),
        ],
        scratch_shapes=[pltpu_vmem((2 * count,) + rest), pltpu_vmem((2 * count,) + rest)],
    )(position, gathered, responses)


def sweep_kernel(h_ref, s_ref, u_ref, out_ref, ratio_ref):
    n = h_ref.shape[0]

    def side(i):
        centre = u_ref[i]
        curve = -2.0 * centre
        if i > 0:
            curve = u_ref[i - 1] + curve
        if i < n - 1:
            curve = curve + u_ref[i + 1]
        return s_ref[i] - h_ref[i] * curve

    ratio = None
    value = None
    for i in range(n):
        hi = h_ref[i]
        if i == 0:
            denom = 1.0 + 2.0 * hi
            value = side(i) / denom
        else:
            denom = 1.0 + 2.0 * hi + hi * ratio
            value = (side(i) + hi * value) / denom
        ratio = -hi / denom
        ratio_ref[i] = ratio
        out_ref[i] = value
    x = value
    for i in range(n - 2, -1, -1):
        x = out_ref[i] - ratio_ref[i] * x
        out_ref[i] = x


def sweep_call(h_lines, d_lines, u_lines):
    return pl.pallas_call(
        sweep_kernel,
        out_shape=jax.ShapeDtypeStruct(h_lines.shape, jnp.float32),
        scratch_shapes=[pltpu_vmem(h_lines.shape)],
    )(h_lines, d_lines, u_lines)


def doubling_gather(part, axis):
    count = lax.axis_size(axis)
    if count & (count - 1):
        return lax.all_gather(part, axis)
    mine = lax.axis_index(axis)
    held = part[None]
    step = 1
    while step < count:
        other = lax.ppermute(held, axis, [(i, i ^ step) for i in range(count)])
        lower = (mine // step) % 2 == 0
        held = jnp.where(
            lower, jnp.concatenate([held, other], 0), jnp.concatenate([other, held], 0)
        )
        step *= 2
    return held


def distributed_solve(h_lines, d_lines, axis, doubling, edges=None):
    responses, reduced = partition_call(h_lines, d_lines, edges)
    if doubling:
        gathered = doubling_gather(reduced, axis)
    else:
        gathered = lax.all_gather(reduced, axis)
    position = jnp.reshape(lax.axis_index(axis), (1,)).astype(jnp.int32)
    return finish_call(gathered, responses, position)


def per_device(initial_heat_values, spreading_coefficients):
    conductivity_map = diffusion_number * spreading_coefficients
    half_rate = implicit_weight * conductivity_map
    plane_count, row_count, column_count = initial_heat_values.shape
    x_low = jnp.zeros_like(initial_heat_values[:, :1])
    x_high = x_low
    y_low, y_high = halos(initial_heat_values, "gy", 2)
    horizontal_implicit_solve = conductivity_map * (
        jnp.concatenate([x_low, initial_heat_values[:, :-1]], 1)
        - 2.0 * initial_heat_values
        + jnp.concatenate([initial_heat_values[:, 1:], x_high], 1)
    )
    vertical_implicit_solve = conductivity_map * (
        jnp.concatenate([y_low, initial_heat_values[:, :, :-1]], 2)
        - 2.0 * initial_heat_values
        + jnp.concatenate([initial_heat_values[:, :, 1:], y_high], 2)
    )
    depth_edge_extension = jnp.pad(initial_heat_values, ((1, 1), (0, 0), (0, 0)))
    depth_implicit_solve = conductivity_map * (
        depth_edge_extension[:-2] - 2.0 * initial_heat_values + depth_edge_extension[2:]
    )
    forward_euler_increment = (
        initial_heat_values
        + horizontal_implicit_solve
        + vertical_implicit_solve
        + depth_implicit_solve
    )
    first_side = jnp.moveaxis(
        forward_euler_increment - implicit_weight * horizontal_implicit_solve, 1, 0
    )
    first_rate = jnp.moveaxis(half_rate, 1, 0)
    first_pass = jnp.moveaxis(distributed_solve(
            first_rate,
            first_side,
            "gx",
            False,
            jnp.stack([initial_heat_values[:, 0], initial_heat_values[:, row_count - 1]], 0),
        ), 0, 1)
    second_side = first_pass - implicit_weight * vertical_implicit_solve
    lanes = 128
    groups = plane_count * row_count // lanes
    side_lines = jnp.transpose(second_side, (2, 0, 1)).reshape(column_count, groups, lanes)
    rate_lines = jnp.transpose(half_rate, (2, 0, 1)).reshape(column_count, groups, lanes)
    column_lines = distributed_solve(rate_lines, side_lines, "gy", True)
    second = jnp.transpose(column_lines.reshape(column_count, plane_count, row_count), (1, 2, 0))
    return sweep_call(half_rate, second, initial_heat_values)


def solution(mesh):
    in_specs = (P(None, "gx", "gy"), P(None, "gx", "gy"))
    out_specs = P(None, "gx", "gy")
    return jax.shard_map(
        per_device, mesh=mesh, in_specs=in_specs, out_specs=out_specs, check_vma=False
    )
```

```python
import functools

import jax
import jax.numpy as jnp
from jax import lax
from jax.experimental import pallas as pl
from jax.experimental.pallas import tpu as pltpu
from jax.sharding import PartitionSpec as P

diffusion_number = 1000.0
implicit_weight = 0.5


def halos(block, axis, dim):
    count = lax.axis_size(axis)
    forward = [(i, i + 1) for i in range(count - 1)]
    backward = [(target, source) for source, target in forward]
    last = lax.index_in_dim(block, block.shape[dim] - 1, dim, keepdims=False)
    first = lax.index_in_dim(block, 0, dim, keepdims=False)
    low = lax.ppermute(last, axis, forward)
    high = lax.ppermute(first, axis, backward)
    return jnp.expand_dims(low, dim), jnp.expand_dims(high, dim)


def partition_kernel(has_edges, has_curve, h_ref, d_ref, *refs):
    refs = list(refs)
    edges_ref = refs.pop(0) if has_edges else None
    if has_curve:
        u_ref, low_ref, high_ref = refs[:3]
        refs = refs[3:]
    out_ref, red_ref, ratio_ref = refs

    def side(i):
        if not has_curve:
            return d_ref[i]
        previous = u_ref[i - 1] if i > 0 else low_ref[...]
        following = u_ref[i + 1] if i < u_ref.shape[0] - 1 else high_ref[...]
        curve = previous - 2.0 * u_ref[i] + following
        return d_ref[i] - h_ref[i] * curve

    n = h_ref.shape[0]
    ratio = jnp.zeros(h_ref.shape[1:], jnp.float32)
    vb = jnp.zeros_like(ratio)
    vf = jnp.zeros_like(ratio)
    for i in range(1, n - 1):
        hi = h_ref[i]
        denom = 1.0 + 2.0 * hi + hi * ratio
        ratio = -hi / denom
        if i == 1:
            vb = side(i) / denom
            vf = hi / denom
        else:
            vb = (side(i) + hi * vb) / denom
            vf = (hi * vf) / denom
        if i == n - 2:
            vl = hi / denom
        ratio_ref[i] = ratio
        out_ref[0, i] = vb
        out_ref[1, i] = vf
    b, f, l = vb, vf, vl
    out_ref[2, n - 2] = l
    for i in range(n - 3, 0, -1):
        r = ratio_ref[i]
        b = out_ref[0, i] - r * b
        f = out_ref[1, i] - r * f
        l = -r * l
        out_ref[0, i] = b
        out_ref[1, i] = f
        out_ref[2, i] = l
    zero = jnp.zeros_like(ratio)
    for k in range(3):
        out_ref[k, 0] = zero
        out_ref[k, n - 1] = zero
    rh = h_ref[0]
    rt = h_ref[n - 1]
    red_ref[0, 0] = -rh
    red_ref[0, 1] = -rt * out_ref[1, n - 2]
    red_ref[1, 0] = 1.0 + 2.0 * rh - rh * out_ref[1, 1]
    red_ref[1, 1] = 1.0 + 2.0 * rt - rt * out_ref[2, n - 2]
    red_ref[2, 0] = -rh * out_ref[2, 1]
    red_ref[2, 1] = -rt
    red_ref[3, 0] = side(0) + rh * out_ref[0, 1]
    red_ref[3, 1] = side(n - 1) + rt * out_ref[0, n - 2]
    if edges_ref is not None:
        red_ref[4, 0] = edges_ref[0]
        red_ref[4, 1] = edges_ref[1]


def partition_call(h_lines, d_lines, edges, curve):
    n = h_lines.shape[0]
    rest = h_lines.shape[1:]
    operands = (h_lines, d_lines)
    if edges is not None:
        operands = operands + (edges,)
    if curve is not None:
        operands = operands + tuple(curve)
    rows = 4 if edges is None else 5
    return pl.pallas_call(
        functools.partial(partition_kernel, edges is not None, curve is not None),
        out_shape=(
            jax.ShapeDtypeStruct((3, n) + rest, jnp.float32),
            jax.ShapeDtypeStruct((rows, 2) + rest, jnp.float32),
        ),
        scratch_shapes=[pltpu_vmem((n,) + rest)],
    )(*operands)


def pltpu_vmem(shape):
    return pltpu.VMEM(shape, jnp.float32)


def finish_kernel(position_ref, g_ref, responses_ref, out_ref, ratio_ref, ends_ref):
    count = g_ref.shape[0]
    n = responses_ref.shape[1]
    ratio = None
    value = None
    for j in range(2 * count):
        k, q = divmod(j, 2)
        lower = g_ref[k, 0, q]
        centre = g_ref[k, 1, q]
        upper = g_ref[k, 2, q]
        side = g_ref[k, 3, q]
        if g_ref.shape[1] == 5 and q == 0 and k > 0:
            side = side - lower * g_ref[k - 1, 4, 1]
        if g_ref.shape[1] == 5 and q == 1 and k < count - 1:
            side = side - upper * g_ref[k + 1, 4, 0]
        if j == 0:
            denom = centre
            value = side / denom
        else:
            denom = centre - lower * ratio
            value = (side - lower * value) / denom
        ratio = upper / denom
        ratio_ref[j] = ratio
        ends_ref[j] = value
    x = value
    for j in range(2 * count - 2, -1, -1):
        x = ends_ref[j] - ratio_ref[j] * x
        ends_ref[j] = x
    mine = position_ref[0]
    head = ends_ref[2 * mine]
    tail = ends_ref[2 * mine + 1]
    out_ref[0] = head
    out_ref[n - 1] = tail
    for i in range(1, n - 1):
        out_ref[i] = responses_ref[0, i] + responses_ref[1, i] * head + responses_ref[2, i] * tail


def finish_call(gathered, responses, position):
    count = gathered.shape[0]
    rest = gathered.shape[3:]
    n = responses.shape[1]
    return pl.pallas_call(
        finish_kernel,
        out_shape=jax.ShapeDtypeStruct((n,) + rest, jnp.float32),
        in_specs=[
            pl.BlockSpec(memory_space=pltpu.SMEM),
            pl.BlockSpec(memory_space=pltpu.VMEM),
            pl.BlockSpec(memory_space=pltpu.VMEM),
        ],
        scratch_shapes=[pltpu_vmem((2 * count,) + rest), pltpu_vmem((2 * count,) + rest)],
    )(position, gathered, responses)


def sweep_kernel(h_ref, s_ref, u_ref, out_ref, ratio_ref):
    n = h_ref.shape[0]

    def side(i):
        centre = u_ref[i]
        curve = -2.0 * centre
        if i > 0:
            curve = u_ref[i - 1] + curve
        if i < n - 1:
            curve = curve + u_ref[i + 1]
        return s_ref[i] - h_ref[i] * curve

    ratio = None
    value = None
    for i in range(n):
        hi = h_ref[i]
        if i == 0:
            denom = 1.0 + 2.0 * hi
            value = side(i) / denom
        else:
            denom = 1.0 + 2.0 * hi + hi * ratio
            value = (side(i) + hi * value) / denom
        ratio = -hi / denom
        ratio_ref[i] = ratio
        out_ref[i] = value
    x = value
    for i in range(n - 2, -1, -1):
        x = out_ref[i] - ratio_ref[i] * x
        out_ref[i] = x


def sweep_call(h_lines, d_lines, u_lines):
    return pl.pallas_call(
        sweep_kernel,
        out_shape=jax.ShapeDtypeStruct(h_lines.shape, jnp.float32),
        scratch_shapes=[pltpu_vmem(h_lines.shape)],
    )(h_lines, d_lines, u_lines)


def doubling_gather(part, axis):
    count = lax.axis_size(axis)
    if count & (count - 1):
        return lax.all_gather(part, axis)
    mine = lax.axis_index(axis)
    held = part[None]
    step = 1
    while step < count:
        other = lax.ppermute(held, axis, [(i, i ^ step) for i in range(count)])
        lower = (mine // step) % 2 == 0
        held = jnp.where(
            lower, jnp.concatenate([held, other], 0), jnp.concatenate([other, held], 0)
        )
        step *= 2
    return held


def distributed_solve(h_lines, d_lines, axis, doubling, edges=None, curve=None):
    responses, reduced = partition_call(h_lines, d_lines, edges, curve)
    if doubling:
        gathered = doubling_gather(reduced, axis)
    else:
        gathered = lax.all_gather(reduced, axis)
    position = jnp.reshape(lax.axis_index(axis), (1,)).astype(jnp.int32)
    return finish_call(gathered, responses, position)


def per_device(initial_heat_values, spreading_coefficients):
    conductivity_map = diffusion_number * spreading_coefficients
    half_rate = implicit_weight * conductivity_map
    plane_count, row_count, column_count = initial_heat_values.shape
    x_low = jnp.zeros_like(initial_heat_values[:, :1])
    x_high = x_low
    lanes = 128
    groups = plane_count * row_count // lanes
    field_lines = jnp.transpose(initial_heat_values, (2, 0, 1)).reshape(
        column_count, groups, lanes
    )
    low_row, high_row = halos(field_lines, "gy", 0)
    y_low = low_row.reshape(plane_count, row_count, 1)
    y_high = high_row.reshape(plane_count, row_count, 1)
    horizontal_implicit_solve = conductivity_map * (
        jnp.concatenate([x_low, initial_heat_values[:, :-1]], 1)
        - 2.0 * initial_heat_values
        + jnp.concatenate([initial_heat_values[:, 1:], x_high], 1)
    )
    vertical_implicit_solve = conductivity_map * (
        jnp.concatenate([y_low, initial_heat_values[:, :, :-1]], 2)
        - 2.0 * initial_heat_values
        + jnp.concatenate([initial_heat_values[:, :, 1:], y_high], 2)
    )
    depth_edge_extension = jnp.pad(initial_heat_values, ((1, 1), (0, 0), (0, 0)))
    depth_implicit_solve = conductivity_map * (
        depth_edge_extension[:-2] - 2.0 * initial_heat_values + depth_edge_extension[2:]
    )
    forward_euler_increment = (
        initial_heat_values
        + horizontal_implicit_solve
        + vertical_implicit_solve
        + depth_implicit_solve
    )
    first_side = jnp.moveaxis(
        forward_euler_increment - implicit_weight * horizontal_implicit_solve, 1, 0
    )
    first_rate = jnp.moveaxis(half_rate, 1, 0)
    first_pass = jnp.moveaxis(distributed_solve(
            first_rate,
            first_side,
            "gx",
            False,
            jnp.stack([initial_heat_values[:, 0], initial_heat_values[:, row_count - 1]], 0),
        ), 0, 1)
    side_lines = jnp.transpose(first_pass, (2, 0, 1)).reshape(column_count, groups, lanes)
    rate_lines = jnp.transpose(half_rate, (2, 0, 1)).reshape(column_count, groups, lanes)
    column_lines = distributed_solve(
        rate_lines,
        side_lines,
        "gy",
        True,
        curve=(field_lines, low_row[0], high_row[0]),
    )
    second = jnp.transpose(column_lines.reshape(column_count, plane_count, row_count), (1, 2, 0))
    return sweep_call(half_rate, second, initial_heat_values)


def solution(mesh):
    in_specs = (P(None, "gx", "gy"), P(None, "gx", "gy"))
    out_specs = P(None, "gx", "gy")
    return jax.shard_map(
        per_device, mesh=mesh, in_specs=in_specs, out_specs=out_specs, check_vma=False
    )
```

```python
import jax
import jax.numpy as jnp
from jax import lax
from jax.experimental import pallas as pl
from jax.experimental.pallas import tpu as pltpu
from jax.sharding import PartitionSpec as P

diffusion_number = 1000.0
implicit_weight = 0.5


def halos(block, axis, dim):
    count = lax.axis_size(axis)
    forward = [(i, i + 1) for i in range(count - 1)]
    backward = [(target, source) for source, target in forward]
    last = lax.index_in_dim(block, block.shape[dim] - 1, dim, keepdims=False)
    first = lax.index_in_dim(block, 0, dim, keepdims=False)
    low = lax.ppermute(last, axis, forward)
    high = lax.ppermute(first, axis, backward)
    return jnp.expand_dims(low, dim), jnp.expand_dims(high, dim)


def partition_kernel(h_ref, d_ref, *refs):
    if len(refs) == 4:
        edges_ref, out_ref, red_ref, ratio_ref = refs
    else:
        edges_ref = None
        out_ref, red_ref, ratio_ref = refs
    n = h_ref.shape[0]
    ratio = jnp.zeros(h_ref.shape[1:], jnp.float32)
    vb = jnp.zeros_like(ratio)
    vf = jnp.zeros_like(ratio)
    for i in range(1, n - 1):
        hi = h_ref[i]
        denom = 1.0 + 2.0 * hi + hi * ratio
        ratio = -hi / denom
        if i == 1:
            vb = d_ref[i] / denom
            vf = hi / denom
        else:
            vb = (d_ref[i] + hi * vb) / denom
            vf = (hi * vf) / denom
        if i == n - 2:
            vl = hi / denom
        ratio_ref[i] = ratio
        out_ref[0, i] = vb
        out_ref[1, i] = vf
    b, f, l = vb, vf, vl
    out_ref[2, n - 2] = l
    for i in range(n - 3, 0, -1):
        r = ratio_ref[i]
        b = out_ref[0, i] - r * b
        f = out_ref[1, i] - r * f
        l = -r * l
        out_ref[0, i] = b
        out_ref[1, i] = f
        out_ref[2, i] = l
    zero = jnp.zeros_like(ratio)
    for k in range(3):
        out_ref[k, 0] = zero
        out_ref[k, n - 1] = zero
    rh = h_ref[0]
    rt = h_ref[n - 1]
    red_ref[0, 0] = -rh
    red_ref[0, 1] = -rt * out_ref[1, n - 2]
    red_ref[1, 0] = 1.0 + 2.0 * rh - rh * out_ref[1, 1]
    red_ref[1, 1] = 1.0 + 2.0 * rt - rt * out_ref[2, n - 2]
    red_ref[2, 0] = -rh * out_ref[2, 1]
    red_ref[2, 1] = -rt
    red_ref[3, 0] = d_ref[0] + rh * out_ref[0, 1]
    red_ref[3, 1] = d_ref[n - 1] + rt * out_ref[0, n - 2]
    if edges_ref is not None:
        red_ref[4, 0] = edges_ref[0]
        red_ref[4, 1] = edges_ref[1]


def partition_call(h_lines, d_lines, edges):
    n = h_lines.shape[0]
    rest = h_lines.shape[1:]
    operands = (h_lines, d_lines) if edges is None else (h_lines, d_lines, edges)
    rows = 4 if edges is None else 5
    return pl.pallas_call(
        partition_kernel,
        out_shape=(
            jax.ShapeDtypeStruct((3, n) + rest, jnp.float32),
            jax.ShapeDtypeStruct((rows, 2) + rest, jnp.float32),
        ),
        scratch_shapes=[pltpu_vmem((n,) + rest)],
    )(*operands)


def pltpu_vmem(shape):
    return pltpu.VMEM(shape, jnp.float32)


def finish_kernel(position_ref, g_ref, responses_ref, out_ref, ratio_ref, ends_ref):
    count = g_ref.shape[0]
    n = responses_ref.shape[1]
    ratio = None
    value = None
    for j in range(2 * count):
        k, q = divmod(j, 2)
        lower = g_ref[k, 0, q]
        centre = g_ref[k, 1, q]
        upper = g_ref[k, 2, q]
        side = g_ref[k, 3, q]
        if g_ref.shape[1] == 5 and q == 0 and k > 0:
            side = side - lower * g_ref[k - 1, 4, 1]
        if g_ref.shape[1] == 5 and q == 1 and k < count - 1:
            side = side - upper * g_ref[k + 1, 4, 0]
        if j == 0:
            denom = centre
            value = side / denom
        else:
            denom = centre - lower * ratio
            value = (side - lower * value) / denom
        ratio = upper / denom
        ratio_ref[j] = ratio
        ends_ref[j] = value
    x = value
    for j in range(2 * count - 2, -1, -1):
        x = ends_ref[j] - ratio_ref[j] * x
        ends_ref[j] = x
    mine = position_ref[0]
    head = ends_ref[2 * mine]
    tail = ends_ref[2 * mine + 1]
    out_ref[0] = head
    out_ref[n - 1] = tail
    for i in range(1, n - 1):
        out_ref[i] = responses_ref[0, i] + responses_ref[1, i] * head + responses_ref[2, i] * tail


def finish_call(gathered, responses, position):
    count = gathered.shape[0]
    rest = gathered.shape[3:]
    n = responses.shape[1]
    return pl.pallas_call(
        finish_kernel,
        out_shape=jax.ShapeDtypeStruct((n,) + rest, jnp.float32),
        in_specs=[
            pl.BlockSpec(memory_space=pltpu.SMEM),
            pl.BlockSpec(memory_space=pltpu.VMEM),
            pl.BlockSpec(memory_space=pltpu.VMEM),
        ],
        scratch_shapes=[pltpu_vmem((2 * count,) + rest), pltpu_vmem((2 * count,) + rest)],
    )(position, gathered, responses)


def sweep_kernel(h_ref, y_ref, u_ref, out_ref, ratio_ref, s_ref):
    n = h_ref.shape[0]
    groups = y_ref.shape[1]
    per = n // groups
    for g in range(groups):
        block = jnp.transpose(y_ref[:, g, :])
        s_ref[g * per : (g + 1) * per] = block.reshape(per, s_ref.shape[1], s_ref.shape[2])

    def side(i):
        centre = u_ref[i]
        curve = -2.0 * centre
        if i > 0:
            curve = u_ref[i - 1] + curve
        if i < n - 1:
            curve = curve + u_ref[i + 1]
        return s_ref[i] - h_ref[i] * curve

    ratio = None
    value = None
    for i in range(n):
        hi = h_ref[i]
        if i == 0:
            denom = 1.0 + 2.0 * hi
            value = side(i) / denom
        else:
            denom = 1.0 + 2.0 * hi + hi * ratio
            value = (side(i) + hi * value) / denom
        ratio = -hi / denom
        ratio_ref[i] = ratio
        out_ref[i] = value
    x = value
    for i in range(n - 2, -1, -1):
        x = out_ref[i] - ratio_ref[i] * x
        out_ref[i] = x


def sweep_call(h_lines, d_lines, u_lines):
    return pl.pallas_call(
        sweep_kernel,
        out_shape=jax.ShapeDtypeStruct(h_lines.shape, jnp.float32),
        scratch_shapes=[pltpu_vmem(h_lines.shape), pltpu_vmem(h_lines.shape)],
    )(h_lines, d_lines, u_lines)


def doubling_gather(part, axis):
    count = lax.axis_size(axis)
    if count & (count - 1):
        return lax.all_gather(part, axis)
    mine = lax.axis_index(axis)
    held = part[None]
    step = 1
    while step < count:
        other = lax.ppermute(held, axis, [(i, i ^ step) for i in range(count)])
        lower = (mine // step) % 2 == 0
        held = jnp.where(
            lower, jnp.concatenate([held, other], 0), jnp.concatenate([other, held], 0)
        )
        step *= 2
    return held


def distributed_solve(h_lines, d_lines, axis, doubling, edges=None):
    responses, reduced = partition_call(h_lines, d_lines, edges)
    if doubling:
        gathered = doubling_gather(reduced, axis)
    else:
        gathered = lax.all_gather(reduced, axis)
    position = jnp.reshape(lax.axis_index(axis), (1,)).astype(jnp.int32)
    return finish_call(gathered, responses, position)


def per_device(initial_heat_values, spreading_coefficients):
    conductivity_map = diffusion_number * spreading_coefficients
    half_rate = implicit_weight * conductivity_map
    plane_count, row_count, column_count = initial_heat_values.shape
    x_low = jnp.zeros_like(initial_heat_values[:, :1])
    x_high = x_low
    y_low, y_high = halos(initial_heat_values, "gy", 2)
    horizontal_implicit_solve = conductivity_map * (
        jnp.concatenate([x_low, initial_heat_values[:, :-1]], 1)
        - 2.0 * initial_heat_values
        + jnp.concatenate([initial_heat_values[:, 1:], x_high], 1)
    )
    vertical_implicit_solve = conductivity_map * (
        jnp.concatenate([y_low, initial_heat_values[:, :, :-1]], 2)
        - 2.0 * initial_heat_values
        + jnp.concatenate([initial_heat_values[:, :, 1:], y_high], 2)
    )
    depth_edge_extension = jnp.pad(initial_heat_values, ((1, 1), (0, 0), (0, 0)))
    depth_implicit_solve = conductivity_map * (
        depth_edge_extension[:-2] - 2.0 * initial_heat_values + depth_edge_extension[2:]
    )
    forward_euler_increment = (
        initial_heat_values
        + horizontal_implicit_solve
        + vertical_implicit_solve
        + depth_implicit_solve
    )
    first_side = jnp.moveaxis(
        forward_euler_increment - implicit_weight * horizontal_implicit_solve, 1, 0
    )
    first_rate = jnp.moveaxis(half_rate, 1, 0)
    first_pass = jnp.moveaxis(distributed_solve(
            first_rate,
            first_side,
            "gx",
            False,
            jnp.stack([initial_heat_values[:, 0], initial_heat_values[:, row_count - 1]], 0),
        ), 0, 1)
    second_side = first_pass - implicit_weight * vertical_implicit_solve
    lanes = 128
    groups = plane_count * row_count // lanes
    side_lines = jnp.transpose(second_side, (2, 0, 1)).reshape(column_count, groups, lanes)
    rate_lines = jnp.transpose(half_rate, (2, 0, 1)).reshape(column_count, groups, lanes)
    column_lines = distributed_solve(rate_lines, side_lines, "gy", True)
    return sweep_call(half_rate, column_lines, initial_heat_values)


def solution(mesh):
    in_specs = (P(None, "gx", "gy"), P(None, "gx", "gy"))
    out_specs = P(None, "gx", "gy")
    return jax.shard_map(
        per_device, mesh=mesh, in_specs=in_specs, out_specs=out_specs, check_vma=False
    )
```

```python
import jax
import jax.numpy as jnp
from jax import lax
from jax.experimental import pallas as pl
from jax.experimental.pallas import tpu as pltpu
from jax.sharding import PartitionSpec as P

diffusion_number = 1000.0
implicit_weight = 0.5


def halos(block, axis, dim):
    count = lax.axis_size(axis)
    forward = [(i, i + 1) for i in range(count - 1)]
    backward = [(target, source) for source, target in forward]
    last = lax.index_in_dim(block, block.shape[dim] - 1, dim, keepdims=False)
    first = lax.index_in_dim(block, 0, dim, keepdims=False)
    low = lax.ppermute(last, axis, forward)
    high = lax.ppermute(first, axis, backward)
    return jnp.expand_dims(low, dim), jnp.expand_dims(high, dim)


def partition_kernel(h_ref, d_ref, *refs):
    if len(refs) == 4:
        edges_ref, out_ref, red_ref, ratio_ref = refs
    elif len(refs) == 5:
        edges_ref = None
        out_ref, red_ref, ratio_ref, hy_ref, dy_ref = refs
        groups = hy_ref.shape[1]
        per = h_ref.shape[0] // groups
        for source, target in ((h_ref, hy_ref), (d_ref, dy_ref)):
            for g in range(groups):
                block = source[g * per : (g + 1) * per].reshape(target.shape[2], target.shape[0])
                target[:, g, :] = jnp.transpose(block)
        h_ref, d_ref = hy_ref, dy_ref
    else:
        edges_ref = None
        out_ref, red_ref, ratio_ref = refs
    n = h_ref.shape[0]
    ratio = jnp.zeros(h_ref.shape[1:], jnp.float32)
    vb = jnp.zeros_like(ratio)
    vf = jnp.zeros_like(ratio)
    for i in range(1, n - 1):
        hi = h_ref[i]
        denom = 1.0 + 2.0 * hi + hi * ratio
        ratio = -hi / denom
        if i == 1:
            vb = d_ref[i] / denom
            vf = hi / denom
        else:
            vb = (d_ref[i] + hi * vb) / denom
            vf = (hi * vf) / denom
        if i == n - 2:
            vl = hi / denom
        ratio_ref[i] = ratio
        out_ref[0, i] = vb
        out_ref[1, i] = vf
    b, f, l = vb, vf, vl
    out_ref[2, n - 2] = l
    for i in range(n - 3, 0, -1):
        r = ratio_ref[i]
        b = out_ref[0, i] - r * b
        f = out_ref[1, i] - r * f
        l = -r * l
        out_ref[0, i] = b
        out_ref[1, i] = f
        out_ref[2, i] = l
    zero = jnp.zeros_like(ratio)
    for k in range(3):
        out_ref[k, 0] = zero
        out_ref[k, n - 1] = zero
    rh = h_ref[0]
    rt = h_ref[n - 1]
    red_ref[0, 0] = -rh
    red_ref[0, 1] = -rt * out_ref[1, n - 2]
    red_ref[1, 0] = 1.0 + 2.0 * rh - rh * out_ref[1, 1]
    red_ref[1, 1] = 1.0 + 2.0 * rt - rt * out_ref[2, n - 2]
    red_ref[2, 0] = -rh * out_ref[2, 1]
    red_ref[2, 1] = -rt
    red_ref[3, 0] = d_ref[0] + rh * out_ref[0, 1]
    red_ref[3, 1] = d_ref[n - 1] + rt * out_ref[0, n - 2]
    if edges_ref is not None:
        red_ref[4, 0] = edges_ref[0]
        red_ref[4, 1] = edges_ref[1]


def partition_call(h_lines, d_lines, edges, y_major=None):
    operands = (h_lines, d_lines) if edges is None else (h_lines, d_lines, edges)
    rows = 4 if edges is None else 5
    shape = h_lines.shape if y_major is None else y_major
    n = shape[0]
    rest = shape[1:]
    scratch = [pltpu_vmem((n,) + rest)]
    if y_major is not None:
        scratch = scratch + [pltpu_vmem(y_major), pltpu_vmem(y_major)]
    return pl.pallas_call(
        partition_kernel,
        out_shape=(
            jax.ShapeDtypeStruct((3, n) + rest, jnp.float32),
            jax.ShapeDtypeStruct((rows, 2) + rest, jnp.float32),
        ),
        scratch_shapes=scratch,
    )(*operands)


def pltpu_vmem(shape):
    return pltpu.VMEM(shape, jnp.float32)


def finish_kernel(position_ref, g_ref, responses_ref, out_ref, ratio_ref, ends_ref):
    count = g_ref.shape[0]
    n = responses_ref.shape[1]
    ratio = None
    value = None
    for j in range(2 * count):
        k, q = divmod(j, 2)
        lower = g_ref[k, 0, q]
        centre = g_ref[k, 1, q]
        upper = g_ref[k, 2, q]
        side = g_ref[k, 3, q]
        if g_ref.shape[1] == 5 and q == 0 and k > 0:
            side = side - lower * g_ref[k - 1, 4, 1]
        if g_ref.shape[1] == 5 and q == 1 and k < count - 1:
            side = side - upper * g_ref[k + 1, 4, 0]
        if j == 0:
            denom = centre
            value = side / denom
        else:
            denom = centre - lower * ratio
            value = (side - lower * value) / denom
        ratio = upper / denom
        ratio_ref[j] = ratio
        ends_ref[j] = value
    x = value
    for j in range(2 * count - 2, -1, -1):
        x = ends_ref[j] - ratio_ref[j] * x
        ends_ref[j] = x
    mine = position_ref[0]
    head = ends_ref[2 * mine]
    tail = ends_ref[2 * mine + 1]
    out_ref[0] = head
    out_ref[n - 1] = tail
    for i in range(1, n - 1):
        out_ref[i] = responses_ref[0, i] + responses_ref[1, i] * head + responses_ref[2, i] * tail


def finish_call(gathered, responses, position):
    count = gathered.shape[0]
    rest = gathered.shape[3:]
    n = responses.shape[1]
    return pl.pallas_call(
        finish_kernel,
        out_shape=jax.ShapeDtypeStruct((n,) + rest, jnp.float32),
        in_specs=[
            pl.BlockSpec(memory_space=pltpu.SMEM),
            pl.BlockSpec(memory_space=pltpu.VMEM),
            pl.BlockSpec(memory_space=pltpu.VMEM),
        ],
        scratch_shapes=[pltpu_vmem((2 * count,) + rest), pltpu_vmem((2 * count,) + rest)],
    )(position, gathered, responses)


def sweep_kernel(h_ref, y_ref, u_ref, out_ref, ratio_ref, s_ref):
    n = h_ref.shape[0]
    groups = y_ref.shape[1]
    per = n // groups
    for g in range(groups):
        block = jnp.transpose(y_ref[:, g, :])
        s_ref[g * per : (g + 1) * per] = block.reshape(per, s_ref.shape[1], s_ref.shape[2])

    def side(i):
        centre = u_ref[i]
        curve = -2.0 * centre
        if i > 0:
            curve = u_ref[i - 1] + curve
        if i < n - 1:
            curve = curve + u_ref[i + 1]
        return s_ref[i] - h_ref[i] * curve

    ratio = None
    value = None
    for i in range(n):
        hi = h_ref[i]
        if i == 0:
            denom = 1.0 + 2.0 * hi
            value = side(i) / denom
        else:
            denom = 1.0 + 2.0 * hi + hi * ratio
            value = (side(i) + hi * value) / denom
        ratio = -hi / denom
        ratio_ref[i] = ratio
        out_ref[i] = value
    x = value
    for i in range(n - 2, -1, -1):
        x = out_ref[i] - ratio_ref[i] * x
        out_ref[i] = x


def sweep_call(h_lines, d_lines, u_lines):
    return pl.pallas_call(
        sweep_kernel,
        out_shape=jax.ShapeDtypeStruct(h_lines.shape, jnp.float32),
        scratch_shapes=[pltpu_vmem(h_lines.shape), pltpu_vmem(h_lines.shape)],
    )(h_lines, d_lines, u_lines)


def doubling_gather(part, axis):
    count = lax.axis_size(axis)
    if count & (count - 1):
        return lax.all_gather(part, axis)
    mine = lax.axis_index(axis)
    held = part[None]
    step = 1
    while step < count:
        other = lax.ppermute(held, axis, [(i, i ^ step) for i in range(count)])
        lower = (mine // step) % 2 == 0
        held = jnp.where(
            lower, jnp.concatenate([held, other], 0), jnp.concatenate([other, held], 0)
        )
        step *= 2
    return held


def distributed_solve(h_lines, d_lines, axis, doubling, edges=None, y_major=None):
    responses, reduced = partition_call(h_lines, d_lines, edges, y_major)
    if doubling:
        gathered = doubling_gather(reduced, axis)
    else:
        gathered = lax.all_gather(reduced, axis)
    position = jnp.reshape(lax.axis_index(axis), (1,)).astype(jnp.int32)
    return finish_call(gathered, responses, position)


def per_device(initial_heat_values, spreading_coefficients):
    conductivity_map = diffusion_number * spreading_coefficients
    half_rate = implicit_weight * conductivity_map
    plane_count, row_count, column_count = initial_heat_values.shape
    x_low = jnp.zeros_like(initial_heat_values[:, :1])
    x_high = x_low
    y_low, y_high = halos(initial_heat_values, "gy", 2)
    horizontal_implicit_solve = conductivity_map * (
        jnp.concatenate([x_low, initial_heat_values[:, :-1]], 1)
        - 2.0 * initial_heat_values
        + jnp.concatenate([initial_heat_values[:, 1:], x_high], 1)
    )
    vertical_implicit_solve = conductivity_map * (
        jnp.concatenate([y_low, initial_heat_values[:, :, :-1]], 2)
        - 2.0 * initial_heat_values
        + jnp.concatenate([initial_heat_values[:, :, 1:], y_high], 2)
    )
    depth_edge_extension = jnp.pad(initial_heat_values, ((1, 1), (0, 0), (0, 0)))
    depth_implicit_solve = conductivity_map * (
        depth_edge_extension[:-2] - 2.0 * initial_heat_values + depth_edge_extension[2:]
    )
    forward_euler_increment = (
        initial_heat_values
        + horizontal_implicit_solve
        + vertical_implicit_solve
        + depth_implicit_solve
    )
    first_side = jnp.moveaxis(
        forward_euler_increment - implicit_weight * horizontal_implicit_solve, 1, 0
    )
    first_rate = jnp.moveaxis(half_rate, 1, 0)
    first_pass = jnp.moveaxis(distributed_solve(
            first_rate,
            first_side,
            "gx",
            False,
            jnp.stack([initial_heat_values[:, 0], initial_heat_values[:, row_count - 1]], 0),
        ), 0, 1)
    second_side = first_pass - implicit_weight * vertical_implicit_solve
    lanes = 128
    groups = plane_count * row_count // lanes
    column_lines = distributed_solve(
        half_rate, second_side, "gy", True, y_major=(column_count, groups, lanes)
    )
    return sweep_call(half_rate, column_lines, initial_heat_values)


def solution(mesh):
    in_specs = (P(None, "gx", "gy"), P(None, "gx", "gy"))
    out_specs = P(None, "gx", "gy")
    return jax.shard_map(
        per_device, mesh=mesh, in_specs=in_specs, out_specs=out_specs, check_vma=False
    )
```

```python
import jax
import jax.numpy as jnp
from jax import lax
from jax.experimental import pallas as pl
from jax.experimental.pallas import tpu as pltpu
from jax.sharding import PartitionSpec as P

diffusion_number = 1000.0
implicit_weight = 0.5


def halos(block, axis, dim):
    count = lax.axis_size(axis)
    forward = [(i, i + 1) for i in range(count - 1)]
    backward = [(target, source) for source, target in forward]
    last = lax.index_in_dim(block, block.shape[dim] - 1, dim, keepdims=False)
    first = lax.index_in_dim(block, 0, dim, keepdims=False)
    low = lax.ppermute(last, axis, forward)
    high = lax.ppermute(first, axis, backward)
    return jnp.expand_dims(low, dim), jnp.expand_dims(high, dim)


def partition_kernel(h_ref, d_ref, *refs):
    if len(refs) == 4:
        edges_ref, out_ref, red_ref, ratio_ref = refs
    elif len(refs) == 5:
        edges_ref = None
        out_ref, red_ref, ratio_ref, hy_ref, dy_ref = refs
        groups = dy_ref.shape[1]
        per = d_ref.shape[0] // groups
        for g in range(groups):
            block = d_ref[g * per : (g + 1) * per].reshape(dy_ref.shape[2], dy_ref.shape[0])
            dy_ref[:, g, :] = jnp.transpose(block)
        d_ref = dy_ref
    else:
        edges_ref = None
        out_ref, red_ref, ratio_ref = refs
    n = h_ref.shape[0]
    ratio = jnp.zeros(h_ref.shape[1:], jnp.float32)
    vb = jnp.zeros_like(ratio)
    vf = jnp.zeros_like(ratio)
    for i in range(1, n - 1):
        hi = h_ref[i]
        denom = 1.0 + 2.0 * hi + hi * ratio
        ratio = -hi / denom
        if i == 1:
            vb = d_ref[i] / denom
            vf = hi / denom
        else:
            vb = (d_ref[i] + hi * vb) / denom
            vf = (hi * vf) / denom
        if i == n - 2:
            vl = hi / denom
        ratio_ref[i] = ratio
        out_ref[0, i] = vb
        out_ref[1, i] = vf
    b, f, l = vb, vf, vl
    out_ref[2, n - 2] = l
    for i in range(n - 3, 0, -1):
        r = ratio_ref[i]
        b = out_ref[0, i] - r * b
        f = out_ref[1, i] - r * f
        l = -r * l
        out_ref[0, i] = b
        out_ref[1, i] = f
        out_ref[2, i] = l
    zero = jnp.zeros_like(ratio)
    for k in range(3):
        out_ref[k, 0] = zero
        out_ref[k, n - 1] = zero
    rh = h_ref[0]
    rt = h_ref[n - 1]
    red_ref[0, 0] = -rh
    red_ref[0, 1] = -rt * out_ref[1, n - 2]
    red_ref[1, 0] = 1.0 + 2.0 * rh - rh * out_ref[1, 1]
    red_ref[1, 1] = 1.0 + 2.0 * rt - rt * out_ref[2, n - 2]
    red_ref[2, 0] = -rh * out_ref[2, 1]
    red_ref[2, 1] = -rt
    red_ref[3, 0] = d_ref[0] + rh * out_ref[0, 1]
    red_ref[3, 1] = d_ref[n - 1] + rt * out_ref[0, n - 2]
    if edges_ref is not None:
        red_ref[4, 0] = edges_ref[0]
        red_ref[4, 1] = edges_ref[1]


def partition_call(h_lines, d_lines, edges, y_major=None):
    operands = (h_lines, d_lines) if edges is None else (h_lines, d_lines, edges)
    rows = 4 if edges is None else 5
    shape = h_lines.shape if y_major is None else y_major
    n = shape[0]
    rest = shape[1:]
    scratch = [pltpu_vmem((n,) + rest)]
    if y_major is not None:
        scratch = scratch + [pltpu_vmem(y_major), pltpu_vmem(y_major)]
    return pl.pallas_call(
        partition_kernel,
        out_shape=(
            jax.ShapeDtypeStruct((3, n) + rest, jnp.float32),
            jax.ShapeDtypeStruct((rows, 2) + rest, jnp.float32),
        ),
        scratch_shapes=scratch,
    )(*operands)


def pltpu_vmem(shape):
    return pltpu.VMEM(shape, jnp.float32)


def finish_kernel(position_ref, g_ref, responses_ref, out_ref, ratio_ref, ends_ref):
    count = g_ref.shape[0]
    n = responses_ref.shape[1]
    ratio = None
    value = None
    for j in range(2 * count):
        k, q = divmod(j, 2)
        lower = g_ref[k, 0, q]
        centre = g_ref[k, 1, q]
        upper = g_ref[k, 2, q]
        side = g_ref[k, 3, q]
        if g_ref.shape[1] == 5 and q == 0 and k > 0:
            side = side - lower * g_ref[k - 1, 4, 1]
        if g_ref.shape[1] == 5 and q == 1 and k < count - 1:
            side = side - upper * g_ref[k + 1, 4, 0]
        if j == 0:
            denom = centre
            value = side / denom
        else:
            denom = centre - lower * ratio
            value = (side - lower * value) / denom
        ratio = upper / denom
        ratio_ref[j] = ratio
        ends_ref[j] = value
    x = value
    for j in range(2 * count - 2, -1, -1):
        x = ends_ref[j] - ratio_ref[j] * x
        ends_ref[j] = x
    mine = position_ref[0]
    head = ends_ref[2 * mine]
    tail = ends_ref[2 * mine + 1]
    out_ref[0] = head
    out_ref[n - 1] = tail
    for i in range(1, n - 1):
        out_ref[i] = responses_ref[0, i] + responses_ref[1, i] * head + responses_ref[2, i] * tail


def finish_call(gathered, responses, position):
    count = gathered.shape[0]
    rest = gathered.shape[3:]
    n = responses.shape[1]
    return pl.pallas_call(
        finish_kernel,
        out_shape=jax.ShapeDtypeStruct((n,) + rest, jnp.float32),
        in_specs=[
            pl.BlockSpec(memory_space=pltpu.SMEM),
            pl.BlockSpec(memory_space=pltpu.VMEM),
            pl.BlockSpec(memory_space=pltpu.VMEM),
        ],
        scratch_shapes=[pltpu_vmem((2 * count,) + rest), pltpu_vmem((2 * count,) + rest)],
    )(position, gathered, responses)


def sweep_kernel(h_ref, y_ref, u_ref, out_ref, ratio_ref, s_ref):
    n = h_ref.shape[0]
    groups = y_ref.shape[1]
    per = n // groups
    for g in range(groups):
        block = jnp.transpose(y_ref[:, g, :])
        s_ref[g * per : (g + 1) * per] = block.reshape(per, s_ref.shape[1], s_ref.shape[2])

    def side(i):
        centre = u_ref[i]
        curve = -2.0 * centre
        if i > 0:
            curve = u_ref[i - 1] + curve
        if i < n - 1:
            curve = curve + u_ref[i + 1]
        return s_ref[i] - h_ref[i] * curve

    ratio = None
    value = None
    for i in range(n):
        hi = h_ref[i]
        if i == 0:
            denom = 1.0 + 2.0 * hi
            value = side(i) / denom
        else:
            denom = 1.0 + 2.0 * hi + hi * ratio
            value = (side(i) + hi * value) / denom
        ratio = -hi / denom
        ratio_ref[i] = ratio
        out_ref[i] = value
    x = value
    for i in range(n - 2, -1, -1):
        x = out_ref[i] - ratio_ref[i] * x
        out_ref[i] = x


def sweep_call(h_lines, d_lines, u_lines):
    return pl.pallas_call(
        sweep_kernel,
        out_shape=jax.ShapeDtypeStruct(h_lines.shape, jnp.float32),
        scratch_shapes=[pltpu_vmem(h_lines.shape), pltpu_vmem(h_lines.shape)],
    )(h_lines, d_lines, u_lines)


def doubling_gather(part, axis):
    count = lax.axis_size(axis)
    if count & (count - 1):
        return lax.all_gather(part, axis)
    mine = lax.axis_index(axis)
    held = part[None]
    step = 1
    while step < count:
        other = lax.ppermute(held, axis, [(i, i ^ step) for i in range(count)])
        lower = (mine // step) % 2 == 0
        held = jnp.where(
            lower, jnp.concatenate([held, other], 0), jnp.concatenate([other, held], 0)
        )
        step *= 2
    return held


def distributed_solve(h_lines, d_lines, axis, doubling, edges=None, y_major=None):
    responses, reduced = partition_call(h_lines, d_lines, edges, y_major)
    if doubling:
        gathered = doubling_gather(reduced, axis)
    else:
        gathered = lax.all_gather(reduced, axis)
    position = jnp.reshape(lax.axis_index(axis), (1,)).astype(jnp.int32)
    return finish_call(gathered, responses, position)


def per_device(initial_heat_values, spreading_coefficients):
    conductivity_map = diffusion_number * spreading_coefficients
    half_rate = implicit_weight * conductivity_map
    plane_count, row_count, column_count = initial_heat_values.shape
    x_low = jnp.zeros_like(initial_heat_values[:, :1])
    x_high = x_low
    y_low, y_high = halos(initial_heat_values, "gy", 2)
    horizontal_implicit_solve = conductivity_map * (
        jnp.concatenate([x_low, initial_heat_values[:, :-1]], 1)
        - 2.0 * initial_heat_values
        + jnp.concatenate([initial_heat_values[:, 1:], x_high], 1)
    )
    vertical_implicit_solve = conductivity_map * (
        jnp.concatenate([y_low, initial_heat_values[:, :, :-1]], 2)
        - 2.0 * initial_heat_values
        + jnp.concatenate([initial_heat_values[:, :, 1:], y_high], 2)
    )
    depth_edge_extension = jnp.pad(initial_heat_values, ((1, 1), (0, 0), (0, 0)))
    depth_implicit_solve = conductivity_map * (
        depth_edge_extension[:-2] - 2.0 * initial_heat_values + depth_edge_extension[2:]
    )
    forward_euler_increment = (
        initial_heat_values
        + horizontal_implicit_solve
        + vertical_implicit_solve
        + depth_implicit_solve
    )
    first_side = jnp.moveaxis(
        forward_euler_increment - implicit_weight * horizontal_implicit_solve, 1, 0
    )
    first_rate = jnp.moveaxis(half_rate, 1, 0)
    first_pass = jnp.moveaxis(distributed_solve(
            first_rate,
            first_side,
            "gx",
            False,
            jnp.stack([initial_heat_values[:, 0], initial_heat_values[:, row_count - 1]], 0),
        ), 0, 1)
    second_side = first_pass - implicit_weight * vertical_implicit_solve
    lanes = 128
    groups = plane_count * row_count // lanes
    rate_lines = jnp.transpose(half_rate, (2, 0, 1)).reshape(column_count, groups, lanes)
    column_lines = distributed_solve(
        rate_lines, second_side, "gy", True, y_major=(column_count, groups, lanes)
    )
    return sweep_call(half_rate, column_lines, initial_heat_values)


def solution(mesh):
    in_specs = (P(None, "gx", "gy"), P(None, "gx", "gy"))
    out_specs = P(None, "gx", "gy")
    return jax.shard_map(
        per_device, mesh=mesh, in_specs=in_specs, out_specs=out_specs, check_vma=False
    )
```

```python
import jax
import jax.numpy as jnp
from jax import lax
from jax.experimental import pallas as pl
from jax.experimental.pallas import tpu as pltpu
from jax.sharding import PartitionSpec as P

diffusion_number = 1000.0
implicit_weight = 0.5


def halos(block, axis, dim):
    count = lax.axis_size(axis)
    forward = [(i, i + 1) for i in range(count - 1)]
    backward = [(target, source) for source, target in forward]
    last = lax.index_in_dim(block, block.shape[dim] - 1, dim, keepdims=False)
    first = lax.index_in_dim(block, 0, dim, keepdims=False)
    low = lax.ppermute(last, axis, forward)
    high = lax.ppermute(first, axis, backward)
    return jnp.expand_dims(low, dim), jnp.expand_dims(high, dim)


def partition_kernel(h_ref, d_ref, *refs):
    if len(refs) == 4:
        edges_ref, out_ref, red_ref, ratio_ref = refs
    else:
        edges_ref = None
        out_ref, red_ref, ratio_ref = refs
    n = h_ref.shape[0]
    ratio = jnp.zeros(h_ref.shape[1:], jnp.float32)
    vb = jnp.zeros_like(ratio)
    vf = jnp.zeros_like(ratio)
    for i in range(1, n - 1):
        hi = h_ref[i]
        denom = 1.0 + 2.0 * hi + hi * ratio
        ratio = -hi / denom
        if i == 1:
            vb = d_ref[i] / denom
            vf = hi / denom
        else:
            vb = (d_ref[i] + hi * vb) / denom
            vf = (hi * vf) / denom
        if i == n - 2:
            vl = hi / denom
        ratio_ref[i] = ratio
        out_ref[0, i] = vb
        out_ref[1, i] = vf
    b, f, l = vb, vf, vl
    out_ref[2, n - 2] = l
    for i in range(n - 3, 0, -1):
        r = ratio_ref[i]
        b = out_ref[0, i] - r * b
        f = out_ref[1, i] - r * f
        l = -r * l
        out_ref[0, i] = b
        out_ref[1, i] = f
        out_ref[2, i] = l
    zero = jnp.zeros_like(ratio)
    for k in range(3):
        out_ref[k, 0] = zero
        out_ref[k, n - 1] = zero
    rh = h_ref[0]
    rt = h_ref[n - 1]
    red_ref[0, 0] = -rh
    red_ref[0, 1] = -rt * out_ref[1, n - 2]
    red_ref[1, 0] = 1.0 + 2.0 * rh - rh * out_ref[1, 1]
    red_ref[1, 1] = 1.0 + 2.0 * rt - rt * out_ref[2, n - 2]
    red_ref[2, 0] = -rh * out_ref[2, 1]
    red_ref[2, 1] = -rt
    red_ref[3, 0] = d_ref[0] + rh * out_ref[0, 1]
    red_ref[3, 1] = d_ref[n - 1] + rt * out_ref[0, n - 2]
    if edges_ref is not None:
        red_ref[4, 0] = edges_ref[0]
        red_ref[4, 1] = edges_ref[1]


def partition_call(h_lines, d_lines, edges):
    n = h_lines.shape[0]
    rest = h_lines.shape[1:]
    operands = (h_lines, d_lines) if edges is None else (h_lines, d_lines, edges)
    rows = 4 if edges is None else 5
    return pl.pallas_call(
        partition_kernel,
        out_shape=(
            jax.ShapeDtypeStruct((3, n) + rest, jnp.float32),
            jax.ShapeDtypeStruct((rows, 2) + rest, jnp.float32),
        ),
        scratch_shapes=[pltpu_vmem((n,) + rest)],
    )(*operands)


def pltpu_vmem(shape):
    return pltpu.VMEM(shape, jnp.float32)


def finish_kernel(position_ref, g_ref, *refs):
    if len(refs) == 5:
        other_ref, responses_ref, out_ref, ratio_ref, ends_ref = refs
        half = g_ref.shape[0]
        count = 2 * half
        first_held = (position_ref[0] // half) % 2 == 0

        def entry(k, f, q):
            if k < half:
                return jnp.where(first_held, g_ref[k, f, q], other_ref[k, f, q])
            return jnp.where(first_held, other_ref[k - half, f, q], g_ref[k - half, f, q])

    else:
        responses_ref, out_ref, ratio_ref, ends_ref = refs
        count = g_ref.shape[0]

        def entry(k, f, q):
            return g_ref[k, f, q]

    n = responses_ref.shape[1]
    ratio = None
    value = None
    for j in range(2 * count):
        k, q = divmod(j, 2)
        lower = entry(k, 0, q)
        centre = entry(k, 1, q)
        upper = entry(k, 2, q)
        side = entry(k, 3, q)
        if g_ref.shape[1] == 5 and q == 0 and k > 0:
            side = side - lower * g_ref[k - 1, 4, 1]
        if g_ref.shape[1] == 5 and q == 1 and k < count - 1:
            side = side - upper * g_ref[k + 1, 4, 0]
        if j == 0:
            denom = centre
            value = side / denom
        else:
            denom = centre - lower * ratio
            value = (side - lower * value) / denom
        ratio = upper / denom
        ratio_ref[j] = ratio
        ends_ref[j] = value
    x = value
    for j in range(2 * count - 2, -1, -1):
        x = ends_ref[j] - ratio_ref[j] * x
        ends_ref[j] = x
    mine = position_ref[0]
    head = ends_ref[2 * mine]
    tail = ends_ref[2 * mine + 1]
    out_ref[0] = head
    out_ref[n - 1] = tail
    for i in range(1, n - 1):
        out_ref[i] = responses_ref[0, i] + responses_ref[1, i] * head + responses_ref[2, i] * tail


def finish_call(gathered, responses, position):
    parts = gathered if isinstance(gathered, tuple) else (gathered,)
    count = sum(part.shape[0] for part in parts)
    rest = parts[0].shape[3:]
    n = responses.shape[1]
    return pl.pallas_call(
        finish_kernel,
        out_shape=jax.ShapeDtypeStruct((n,) + rest, jnp.float32),
        in_specs=[pl.BlockSpec(memory_space=pltpu.SMEM)]
        + [pl.BlockSpec(memory_space=pltpu.VMEM)] * (len(parts) + 1),
        scratch_shapes=[pltpu_vmem((2 * count,) + rest), pltpu_vmem((2 * count,) + rest)],
    )(position, *parts, responses)


def sweep_kernel(h_ref, y_ref, u_ref, out_ref, ratio_ref, s_ref):
    n = h_ref.shape[0]
    groups = y_ref.shape[1]
    per = n // groups
    for g in range(groups):
        block = jnp.transpose(y_ref[:, g, :])
        s_ref[g * per : (g + 1) * per] = block.reshape(per, s_ref.shape[1], s_ref.shape[2])

    def side(i):
        centre = u_ref[i]
        curve = -2.0 * centre
        if i > 0:
            curve = u_ref[i - 1] + curve
        if i < n - 1:
            curve = curve + u_ref[i + 1]
        return s_ref[i] - h_ref[i] * curve

    ratio = None
    value = None
    for i in range(n):
        hi = h_ref[i]
        if i == 0:
            denom = 1.0 + 2.0 * hi
            value = side(i) / denom
        else:
            denom = 1.0 + 2.0 * hi + hi * ratio
            value = (side(i) + hi * value) / denom
        ratio = -hi / denom
        ratio_ref[i] = ratio
        out_ref[i] = value
    x = value
    for i in range(n - 2, -1, -1):
        x = out_ref[i] - ratio_ref[i] * x
        out_ref[i] = x


def sweep_call(h_lines, d_lines, u_lines):
    return pl.pallas_call(
        sweep_kernel,
        out_shape=jax.ShapeDtypeStruct(h_lines.shape, jnp.float32),
        scratch_shapes=[pltpu_vmem(h_lines.shape), pltpu_vmem(h_lines.shape)],
    )(h_lines, d_lines, u_lines)


def doubling_gather(part, axis):
    count = lax.axis_size(axis)
    if count & (count - 1):
        return lax.all_gather(part, axis)
    if count == 1:
        return part[None]
    mine = lax.axis_index(axis)
    held = part[None]
    step = 1
    while 2 * step < count:
        other = lax.ppermute(held, axis, [(i, i ^ step) for i in range(count)])
        lower = (mine // step) % 2 == 0
        held = jnp.where(
            lower, jnp.concatenate([held, other], 0), jnp.concatenate([other, held], 0)
        )
        step *= 2
    other = lax.ppermute(held, axis, [(i, i ^ step) for i in range(count)])
    return held, other


def distributed_solve(h_lines, d_lines, axis, doubling, edges=None):
    responses, reduced = partition_call(h_lines, d_lines, edges)
    if doubling:
        gathered = doubling_gather(reduced, axis)
    else:
        gathered = lax.all_gather(reduced, axis)
    position = jnp.reshape(lax.axis_index(axis), (1,)).astype(jnp.int32)
    return finish_call(gathered, responses, position)


def per_device(initial_heat_values, spreading_coefficients):
    conductivity_map = diffusion_number * spreading_coefficients
    half_rate = implicit_weight * conductivity_map
    plane_count, row_count, column_count = initial_heat_values.shape
    x_low = jnp.zeros_like(initial_heat_values[:, :1])
    x_high = x_low
    y_low, y_high = halos(initial_heat_values, "gy", 2)
    horizontal_implicit_solve = conductivity_map * (
        jnp.concatenate([x_low, initial_heat_values[:, :-1]], 1)
        - 2.0 * initial_heat_values
        + jnp.concatenate([initial_heat_values[:, 1:], x_high], 1)
    )
    vertical_implicit_solve = conductivity_map * (
        jnp.concatenate([y_low, initial_heat_values[:, :, :-1]], 2)
        - 2.0 * initial_heat_values
        + jnp.concatenate([initial_heat_values[:, :, 1:], y_high], 2)
    )
    depth_edge_extension = jnp.pad(initial_heat_values, ((1, 1), (0, 0), (0, 0)))
    depth_implicit_solve = conductivity_map * (
        depth_edge_extension[:-2] - 2.0 * initial_heat_values + depth_edge_extension[2:]
    )
    forward_euler_increment = (
        initial_heat_values
        + horizontal_implicit_solve
        + vertical_implicit_solve
        + depth_implicit_solve
    )
    first_side = jnp.moveaxis(
        forward_euler_increment - implicit_weight * horizontal_implicit_solve, 1, 0
    )
    first_rate = jnp.moveaxis(half_rate, 1, 0)
    first_pass = jnp.moveaxis(distributed_solve(
            first_rate,
            first_side,
            "gx",
            False,
            jnp.stack([initial_heat_values[:, 0], initial_heat_values[:, row_count - 1]], 0),
        ), 0, 1)
    second_side = first_pass - implicit_weight * vertical_implicit_solve
    lanes = 128
    groups = plane_count * row_count // lanes
    side_lines = jnp.transpose(second_side, (2, 0, 1)).reshape(column_count, groups, lanes)
    rate_lines = jnp.transpose(half_rate, (2, 0, 1)).reshape(column_count, groups, lanes)
    column_lines = distributed_solve(rate_lines, side_lines, "gy", True)
    return sweep_call(half_rate, column_lines, initial_heat_values)


def solution(mesh):
    in_specs = (P(None, "gx", "gy"), P(None, "gx", "gy"))
    out_specs = P(None, "gx", "gy")
    return jax.shard_map(
        per_device, mesh=mesh, in_specs=in_specs, out_specs=out_specs, check_vma=False
    )
```
